128 devices in a mesh: dp: 4 (over y), tensor: 32 (over x, z, core).
Axes of the slice: x: 4, y: 4, z: 4, core: 2. Of those that a mesh axis runs over, the one named last changes fastest.
Arguments:
- page_pool: bfloat16 [768, 1024, 256], P('dp', 'tensor'), may hold values from -5 to 5
- page_table: int32 [16, 64], P('dp'), may hold values from 0 to 191, as said below
- destination: int32 [16], replicated, may hold values from 0 to 15, as said below
- cache_len: int32 [16], replicated, may hold values from 2048 to 4096, as said below
- new_tokens: bfloat16 [16, 8192, 384], P('dp', 'tensor'), may hold values from -32 to 32
- residual_in: bfloat16 [8192, 2048], P(('dp', 'tensor')), may hold values from -48 to 48
- out_weight: bfloat16 [2048, 2048], P('tensor'), may hold values from -0.5 to 0.5
- norm_gain: float32 [2048], replicated, may hold values from 0.5 to 1.5
- routes: int32 [8192, 6], P(('dp', 'tensor')), may hold values from 0 to 63, all different within a row; in each aligned block of 64 rows (0 to 63, 64 to 127, ...) at most 8 rows name the same one
- route_gates: float32 [8192, 6], P(('dp', 'tensor')), may hold values from 0.1 to 1
- expert_gate: bfloat16 [64, 2048, 1408], P('tensor', None, 'dp'), may hold values from -0.125 to 0.125
- expert_up: bfloat16 [64, 2048, 1408], P('tensor', None, 'dp'), may hold values from -0.125 to 0.125
- expert_down: bfloat16 [64, 1408, 2048], P('tensor', 'dp'), may hold values from -0.15625 to 0.15625
Outputs:
- layer_out: float32 [8192, 2048], P(('dp', 'tensor'))
The draws below stay inside these ranges and needn't reach their ends.
Inputs may be any that keep to these rules, and one draw needn't show every extreme that they name: `page_table`: each request names pages of its own dp index's pool of 192 pages; requests 2m and 2m + 1 of a dp index share the first half of their 64 pages, and no other page is named twice within a dp index. `destination`: A permutation of the serving slots; each dp index sends exactly one of its 4 requests to a slot of each other dp index and keeps the others in their own slots. `cache_len`: some request has exactly 4096 cached positions. `routes`: in the rows of one device (64 tokens) no expert is named more than 8 times.
All inputs are finite; a program needn't handle non-finite values.
Results may differ from the reference program's by a relative error of at most 0.004.
Values may be sent and summed in bfloat16 or wider, within the bound.
No kernel may reach another device: no remote copies, remote signals or barrier semaphores. Data moves between devices by JAX's collectives and lax.ppermute only.
A program may use at most 128 MiB of HBM per device.

```python
import math
import jax
import jax.numpy as jnp
import numpy as np
from jax import lax

D = 2048
HEADS = 16
HD = 128
EXPERTS = 64
FFE = 1408
TOP = 6
SPAN = 512
REQ_DEV = 4
PAGE = 64
PAGES_REQ = 64
REQUESTS = 16
TOKENS = 8192
TOK_DEV = 64
CACHE = 4096
POOL = 192
CAP = 8
FFE_DEV = 352
N_DP = 4


def draw_page_table(key, part):
    half_pages = PAGES_REQ // 2
    group_keys = jax.random.split(key, N_DP)

    def one_group(group_key):
        return jax.random.permutation(group_key, POOL)
    shuffled = jax.vmap(one_group)(group_keys).reshape(N_DP, REQ_DEV // 2, 3, half_pages)
    prefix = shuffled[:, :, 0]
    first_table = jnp.concatenate([prefix, shuffled[:, :, 1]], axis=2)
    second_table = jnp.concatenate([prefix, shuffled[:, :, 2]], axis=2)
    table = jnp.stack([first_table, second_table], axis=2)
    return table.reshape(REQUESTS, PAGES_REQ).astype(jnp.int32)


def draw_destination(key, part):
    group_keys = jax.random.split(key, N_DP)

    def one_group(group_key):
        return jax.random.permutation(group_key, REQ_DEV)
    order = jax.vmap(one_group)(group_keys).astype(jnp.int32)
    group_ids = jnp.arange(N_DP, dtype=jnp.int32)
    steps_ids = jnp.arange(N_DP - 1, dtype=jnp.int32)
    staying = group_ids[:, None] * REQ_DEV + jnp.arange(REQ_DEV, dtype=jnp.int32)[None, :]
    target = (group_ids[:, None] + 1 + steps_ids[None, :]) % N_DP
    target_slot = order[target, steps_ids[None, :]]
    movers = order[:, :N_DP - 1]
    moved = staying.at[group_ids[:, None], movers].set(target * REQ_DEV + target_slot)
    return moved.reshape(REQUESTS).astype(jnp.int32)


def draw_cache_len(key, part):
    key_lengths, key_pick = jax.random.split(key)
    lengths = jax.random.randint(key_lengths, (REQUESTS,), CACHE // 2, CACHE + 1).astype(jnp.int32)
    longest = jax.random.randint(key_pick, (), 0, REQUESTS)
    return lengths.at[longest].set(CACHE).astype(jnp.int32)


def draw_new_tokens(key, part):
    key_query, key_keys, key_values = jax.random.split(key, 3)
    shape = (REQUESTS, HEADS, SPAN, HD)
    queries = jnp.clip(2.0 * jax.random.normal(key_query, shape, jnp.float32), -8.0, 8.0)
    keys_drawn = jnp.clip(jax.random.normal(key_keys, shape, jnp.float32), -5.0, 5.0)
    values = jnp.clip(jax.random.normal(key_values, shape, jnp.float32), -5.0, 5.0)
    stacked = jnp.concatenate([queries, keys_drawn, values], axis=3)
    return stacked.reshape(REQUESTS, HEADS * SPAN, 3 * HD).astype(jnp.bfloat16)


def draw_residual_in(key, part):
    key_rows, key_cols, key_values = jax.random.split(key, 3)
    col_scale = jnp.exp(jax.random.uniform(key_cols, (1, D), jnp.float32, math.log(0.3), math.log(3.0)))
    row_scale = jnp.exp(jax.random.uniform(key_rows, (TOKENS, 1), jnp.float32, math.log(0.4), math.log(4.0)))
    values = jnp.clip(jax.random.normal(key_values, (TOKENS, D), jnp.float32), -4.0, 4.0)
    return (values * col_scale * row_scale).astype(jnp.bfloat16)


def steps_of(key, extent, shards, low, high):
    loudness, own = 1.0, jax.random.fold_in(key, 6)
    for dim, shards_of in shards:
        draws = jnp.exp(jax.random.uniform(jax.random.fold_in(own, dim), (shards_of,), jnp.float32, low / len(shards), high / len(shards)))
        loudness = loudness * jnp.repeat(draws, extent[dim] // shards_of).reshape([-1 if axis == dim else 1 for axis in range(len(extent))])
    return loudness


def assign_block(stream_key, own, number, rows, amount, top, bound, slope):
    sequence = jax.random.permutation(stream_key, amount)
    packed, common = shares(amount, rows * top, bound, slope, True), shares(amount, rows * top, bound, slope, False)
    places = jnp.arange(amount)

    def named(tallies, turn):
        used = int((tallies > 0).sum())
        fixed = max(1, used // 4)
        passed = fixed + (places - fixed + turn * (used - fixed)) % max(1, amount - fixed)
        return jnp.zeros((amount,), jnp.int32).at[sequence[jnp.where(places < fixed, places, passed)]].set(jnp.asarray(tallies, jnp.int32))

    tallies = jnp.where(number % 4 == 0, named(packed, number // 4), named(common, number - number // 4 - 1))
    mixed = jax.random.permutation(jax.random.fold_in(own, 3), amount)
    donor, receiver = mixed[0:amount // 2 * 2:2], mixed[1:amount // 2 * 2:2]
    room = jnp.minimum(tallies[donor] - 1, bound - tallies[receiver]) // 2
    room = jnp.where((donor == sequence[0]) | (receiver == sequence[0]) | (tallies[receiver] == 0), 0, jnp.maximum(room, 0))
    passed = jax.random.randint(jax.random.fold_in(own, 4), (amount // 2,), 0, 1 << 20) % (room + 1)
    tallies = tallies.at[donor].add(-passed).at[receiver].add(passed)
    items = jnp.searchsorted(jnp.cumsum(tallies), jnp.arange(rows * top), side="right").astype(jnp.int32)
    table = items.reshape(top, rows).T
    table = table[jax.random.permutation(jax.random.fold_in(own, 1), rows)]
    turn = jax.random.randint(jax.random.fold_in(own, 2), (rows, 1), 0, top)
    return jnp.take_along_axis(table, (jnp.arange(top)[None, :] + turn) % top, axis=1)


def shares(count, total, bound, skew, full):
    weights = [(1 << 20) // math.isqrt(rank ** skew) + 1 for rank in range(1, count + 1)]
    largest = bound if full else min(bound, max(-(-total // count), total * weights[0] // sum(weights)))
    least = 1 if total - largest >= count - 1 else 0
    given, rest = [largest] + [least] * (count - 1), total - largest - least * (count - 1)
    while rest > 0:
        candidates = [i for i in range(1, count) if given[i] < largest] or [i for i in range(1, count) if given[i] < bound]
        pool, remaining = sum([weights[i] for i in candidates]), rest
        for i in candidates:
            addition = min(bound - given[i], max(1, remaining * weights[i] // pool), rest)
            given[i] = given[i] + addition
            rest = rest - addition
    return np.array(given)


def scatter_about(rng, dims, scale, most, cuts=(), held_as=jnp.bfloat16):
    gain = steps_of(rng, dims, cuts, -0.22, 0.18) if cuts else 1.0
    values = jax.random.normal(rng, dims, jnp.float32) * scale * gain
    return jnp.minimum(jnp.maximum(values, -most), most).astype(held_as)


def setup_inputs(seed: int = 0) -> dict:
    keys = jax.random.split(jax.random.key(seed), 14)
    page_pool = scatter_about(keys[0], (N_DP * POOL, HEADS * PAGE, 2 * HD), 1.0, 5.0, ((0, 4), (1, 32)))
    page_table = draw_page_table(jax.random.fold_in(keys[13], 71), 0)
    destination = draw_destination(jax.random.fold_in(keys[13], 71), 0)
    cache_len = draw_cache_len(jax.random.fold_in(keys[13], 71), 0)
    new_tokens = draw_new_tokens(jax.random.fold_in(keys[13], 71), 0)
    residual_in = draw_residual_in(jax.random.fold_in(keys[13], 71), 0)
    out_weight = scatter_about(keys[6], (HEADS * HD, D), HD ** -0.5, 0.5, ((0, 32),))
    norm_gain = jnp.clip(1.0 + 0.1 * jax.random.normal(keys[7], (D,), jnp.float32), 0.5, 1.5)
    routes_keys = jax.random.split(jax.random.fold_in(keys[8], 1), TOKENS // TOK_DEV)
    routes_turns = jax.random.permutation(jax.random.fold_in(keys[8], 3), TOKENS // TOK_DEV)
    routes = jax.vmap(lambda own, number: assign_block(jax.random.fold_in(keys[8], 2), own, number, TOK_DEV, EXPERTS, TOP, CAP, 2))(routes_keys, routes_turns).reshape((TOKENS, TOP))
    route_gates = jnp.clip(jnp.exp(math.log(1.0) - 2.3025851 * jax.random.uniform(keys[9], (TOKENS, TOP), jnp.float32) ** steps_of(keys[9], (TOKENS, TOP), ((0, 128),), -0.2, 0.2)), 0.1, 1.0)
    expert_gate = scatter_about(keys[10], (EXPERTS, D, FFE), D ** -0.5, 0.125, ((0, 32), (2, 4)))
    expert_up = scatter_about(keys[11], (EXPERTS, D, FFE), D ** -0.5, 0.125, ((0, 32), (2, 4)))
    expert_down = scatter_about(keys[12], (EXPERTS, FFE, D), FFE ** -0.5, 0.15625, ((0, 32), (1, 4)))
    return {"page_pool": page_pool, "page_table": page_table, "destination": destination, "cache_len": cache_len, "new_tokens": new_tokens, "residual_in": residual_in, "out_weight": out_weight, "norm_gain": norm_gain, "routes": routes, "route_gates": route_gates, "expert_gate": expert_gate, "expert_up": expert_up, "expert_down": expert_down}


def attend_head(cached, fresh_rows, length):
    queries = fresh_rows[:, :HD]
    new_keys = fresh_rows[:, HD:2 * HD]
    new_values = fresh_rows[:, 2 * HD:]
    scale_factor = 1.0 / HD ** 0.5
    cache_scores = jnp.dot(queries, cached[:, :HD].T, preferred_element_type=jnp.float32) * scale_factor
    span_scores = jnp.dot(queries, new_keys.T, preferred_element_type=jnp.float32) * scale_factor
    cache_live = jnp.arange(CACHE, dtype=jnp.int32)[None, :] < length
    positions = jnp.arange(SPAN, dtype=jnp.int32)
    span_live = positions[None, :] <= positions[:, None]
    cache_scores = jnp.where(cache_live, cache_scores, -1e+30)
    span_scores = jnp.where(span_live, span_scores, -1e+30)
    maximum = jnp.maximum(lax.optimization_barrier(jnp.max(cache_scores, axis=1)), lax.optimization_barrier(jnp.max(span_scores, axis=1)))
    cache_weights = jnp.exp(cache_scores - maximum[:, None])
    span_weights = jnp.exp(span_scores - maximum[:, None])
    denominator = lax.optimization_barrier(jnp.sum(cache_weights, axis=1)) + lax.optimization_barrier(jnp.sum(span_weights, axis=1))
    weighted = jnp.dot(cache_weights.astype(jnp.bfloat16), cached[:, HD:], preferred_element_type=jnp.float32)
    weighted = weighted + jnp.dot(span_weights.astype(jnp.bfloat16), new_values, preferred_element_type=jnp.float32)
    return (weighted / denominator[:, None]).astype(jnp.bfloat16)

def reference(page_pool, page_table, destination, cache_len, new_tokens, residual_in, out_weight, norm_gain, routes, route_gates, expert_gate, expert_up, expert_down):
    slot_ids = jnp.arange(REQUESTS, dtype=jnp.int32)
    inverse = jnp.zeros((REQUESTS,), jnp.int32).at[destination].set(slot_ids)

    def one_slot(slot_index):
        home_request = inverse[slot_index]
        home_group = home_request // REQ_DEV
        gathered = page_pool[home_group * POOL + page_table[home_request]]
        cached = gathered.reshape(PAGES_REQ, HEADS, PAGE, 2 * HD).transpose(1, 0, 2, 3).reshape(HEADS, CACHE, 2 * HD)
        fresh_rows = new_tokens[slot_index].reshape(HEADS, SPAN, 3 * HD)
        length = cache_len[home_request]

        def one_head(operands):
            return attend_head(operands[0], operands[1], length)
        heads_out = lax.map(one_head, (cached, fresh_rows))
        return heads_out.transpose(1, 0, 2).reshape(SPAN, HEADS * HD)
    attended = lax.map(one_slot, slot_ids).reshape(TOKENS, HEADS * HD)
    projected = jnp.dot(attended, out_weight, preferred_element_type=jnp.float32)
    hidden = residual_in.astype(jnp.float32) + projected
    normed = (hidden * lax.rsqrt(lax.optimization_barrier(jnp.mean(hidden * hidden, axis=1, keepdims=True)) + 1e-06) * norm_gain).astype(jnp.bfloat16)
    flat_routes = routes.reshape(-1)
    flat_gates = route_gates.reshape(-1)
    most_rows = CAP * (TOKENS // TOK_DEV)

    def add_expert(running, expert):
        named = flat_routes == expert
        pair_hits = jnp.nonzero(named, size=most_rows, fill_value=0)[0].astype(jnp.int32)
        live_rows = jnp.arange(most_rows, dtype=jnp.int32) < jnp.sum(named.astype(jnp.int32))
        token_ids = pair_hits // TOP
        chosen_rows = normed[token_ids]
        gate_part = jnp.dot(chosen_rows, expert_gate[expert], preferred_element_type=jnp.float32)
        up_part = jnp.dot(chosen_rows, expert_up[expert], preferred_element_type=jnp.float32)
        active = (jax.nn.silu(gate_part) * up_part).astype(jnp.bfloat16)
        blocks = active.reshape(most_rows, N_DP, FFE_DEV).astype(jnp.float32)
        down_blocks = expert_down[expert].reshape(N_DP, FFE_DEV, D).astype(jnp.float32)
        partial_value = jnp.einsum('rbf,bfd->rbd', blocks, down_blocks)
        rounded = lax.optimization_barrier(partial_value.astype(jnp.bfloat16))
        expert_out = lax.optimization_barrier(jnp.sum(rounded.astype(jnp.float32), axis=1))
        gate_weight = jnp.where(live_rows, flat_gates[pair_hits], 0.0)
        running = running.at[token_ids].add(gate_weight[:, None] * expert_out)
        return (running, expert)
    routed = lax.scan(add_expert, jnp.zeros((TOKENS, D), jnp.float32), jnp.arange(EXPERTS, dtype=jnp.int32))[0]
    return (hidden + routed).astype(jnp.float32)
```

```python
import jax
import jax.numpy as jnp
from jax import lax
from jax.sharding import PartitionSpec as P

HEADS = 16
HD = 128
EXPERTS = 64
TOP = 6
PAGE = 64


def swapped(array, axis, stride):
    return lax.ppermute(array, axis, [(i, i ^ 1 << stride) for i in range(lax.axis_size(axis))])


def local_attention(queries, cached, fresh_rows, length, cache_offset, span_offset):
    head_size = queries.shape[1]
    span_len = queries.shape[0]
    page_count = cached.shape[0]
    page_rows = cached.shape[1]
    scale_factor = 1.0 / head_size**0.5
    cache_scores = jnp.einsum(
        "qd,pjd->qpj", queries, cached[:, :, :head_size], preferred_element_type=jnp.float32
    )
    cache_scores = cache_scores.reshape(span_len, page_count * page_rows) * scale_factor
    page_ids = jnp.arange(page_count, dtype=jnp.int32)[:, None]
    row_ids = jnp.arange(page_rows, dtype=jnp.int32)[None, :]
    positions = (page_ids * PAGE + cache_offset + row_ids).reshape(-1)
    cache_scores = jnp.where(positions[None, :] < length, cache_scores, -1e30)
    new_keys = fresh_rows[:, head_size : 2 * head_size]
    new_values = fresh_rows[:, 2 * head_size :]
    span_scores = jnp.dot(queries, new_keys.T, preferred_element_type=jnp.float32) * scale_factor
    key_pos = span_offset + jnp.arange(fresh_rows.shape[0], dtype=jnp.int32)
    query_pos = jnp.arange(span_len, dtype=jnp.int32)
    span_scores = jnp.where(key_pos[None, :] <= query_pos[:, None], span_scores, -1e30)
    maximum = jnp.maximum(jnp.max(cache_scores, axis=1), jnp.max(span_scores, axis=1))
    cache_weights = jnp.exp(cache_scores - maximum[:, None])
    span_weights = jnp.exp(span_scores - maximum[:, None])
    denominator = jnp.sum(cache_weights, axis=1) + jnp.sum(span_weights, axis=1)
    rounded = cache_weights.astype(jnp.bfloat16).reshape(span_len, page_count, page_rows)
    weighted = jnp.einsum(
        "qpj,pjd->qd", rounded, cached[:, :, head_size:], preferred_element_type=jnp.float32
    )
    weighted = weighted + jnp.dot(
        span_weights.astype(jnp.bfloat16), new_values, preferred_element_type=jnp.float32
    )
    return (weighted, maximum, denominator)


def run_experts(slot_rows, expert_gate, expert_up, expert_down):
    gate_part = jnp.einsum(
        "secd,edf->secf", slot_rows, expert_gate, preferred_element_type=jnp.float32
    )
    up_part = jnp.einsum("secd,edf->secf", slot_rows, expert_up, preferred_element_type=jnp.float32)
    active = (jax.nn.silu(gate_part) * up_part).astype(jnp.bfloat16)
    return jnp.einsum("secf,efd->secd", active, expert_down, preferred_element_type=jnp.float32)


def shards(
    page_pool,
    page_table,
    destination,
    cache_len,
    new_tokens,
    residual_in,
    out_weight,
    norm_gain,
    routes,
    route_gates,
    expert_gate,
    expert_up,
    expert_down,
):
    tensor_size = lax.axis_size("tensor")
    group_count = lax.axis_size("dp")
    split_ways = max(1, tensor_size // HEADS)
    heads_here = max(1, HEADS // tensor_size)
    side_index = lax.axis_index("tensor") % split_ways
    group_index = lax.axis_index("dp")
    requests_here = page_table.shape[0]
    first_home = group_index * requests_here
    home_dest = lax.dynamic_slice_in_dim(destination, first_home, requests_here)
    dest_group = home_dest // requests_here
    group_ids = jnp.arange(group_count, dtype=jnp.int32)
    request_ids = jnp.arange(requests_here, dtype=jnp.int32)
    leaving = dest_group[None, :] == group_ids[:, None]
    chosen = jnp.sum(jnp.where(leaving, request_ids[None, :], 0), axis=1)
    chosen = jnp.where(group_ids == group_index, 0, chosen)
    outgoing = page_pool[page_table[chosen]]
    arrived = lax.all_to_all(outgoing, "dp", split_axis=0, concat_axis=0, tiled=True)
    inverse = (
        jnp.zeros_like(destination)
        .at[destination]
        .set(jnp.arange(destination.shape[0], dtype=jnp.int32))
    )
    served = lax.dynamic_slice_in_dim(inverse, first_home, requests_here)
    source = served // requests_here
    resident = source == group_index
    local_pages = page_pool[page_table[jnp.where(resident, served - first_home, 0)]]
    dense_cache = jnp.where(resident[:, None, None, None], local_pages, arrived[source])
    lengths = cache_len[served]
    fresh_per = new_tokens.shape[1] // heads_here
    span_len = fresh_per * split_ways
    rows_per_head = dense_cache.shape[2] // heads_here
    own_queries = new_tokens[:, :, :HD]
    other_queries = swapped(own_queries, "tensor", 0)
    lower_half = jnp.where(side_index == 0, own_queries, other_queries)
    upper_half = jnp.where(side_index == 0, other_queries, own_queries)
    queries = jnp.concatenate([lower_half, upper_half], axis=1)[:, None]

    def one_request(operands):
        return local_attention(
            operands[0],
            operands[1],
            operands[2],
            operands[3],
            side_index * rows_per_head,
            side_index * fresh_per,
        )

    head_results = lax.map(one_request, (queries[:, 0], dense_cache, new_tokens, lengths))
    weighted, maximum, denominator = head_results
    half_dim = HD // 2
    given_part = lax.dynamic_slice_in_dim(weighted, (1 - side_index) * half_dim, half_dim, 2)
    kept_part = lax.dynamic_slice_in_dim(weighted, side_index * half_dim, half_dim, 2)
    received_part, other_max, other_den = swapped((given_part, maximum, denominator), "tensor", 0)
    joint_max = jnp.maximum(maximum, other_max)
    own_scale = jnp.exp(maximum - joint_max)
    theirs = jnp.exp(other_max - joint_max)
    combined = kept_part * own_scale[..., None] + received_part * theirs[..., None]
    attended = combined / (denominator * own_scale + other_den * theirs)[..., None]
    tok_rows = residual_in.shape[0]
    head_out = attended.astype(jnp.bfloat16).reshape(tensor_size, tok_rows, half_dim)
    owned = lax.all_to_all(head_out, "tensor", split_axis=0, concat_axis=0, tiled=True)
    owned = owned.transpose(1, 0, 2).reshape(tok_rows, tensor_size * half_dim)
    full_weight = lax.all_gather(out_weight, "tensor", axis=0, tiled=True)
    projected = jnp.dot(owned, full_weight, preferred_element_type=jnp.float32)
    hidden = residual_in.astype(jnp.float32) + projected
    normed = (
        hidden * lax.rsqrt(jnp.mean(hidden * hidden, axis=1, keepdims=True) + 1e-06) * norm_gain
    ).astype(jnp.bfloat16)
    capacity = max(2, tok_rows * TOP * 4 // (3 * EXPERTS))
    flat_routes = routes.reshape(-1)
    pair_count = flat_routes.shape[0]
    expert_ids = jnp.arange(EXPERTS, dtype=jnp.int32)
    one_hot = (flat_routes[:, None] == expert_ids[None, :]).astype(jnp.int32)
    earlier = jnp.cumsum(one_hot, axis=0) - one_hot
    rank_in_expert = jnp.sum(earlier * one_hot, axis=1)
    slot_of_pair = flat_routes * capacity + rank_in_expert
    slot_ids = jnp.arange(EXPERTS * capacity, dtype=jnp.int32)
    matches = slot_of_pair[None, :] == slot_ids[:, None]
    source_pair = jnp.sum(
        jnp.where(matches, jnp.arange(pair_count, dtype=jnp.int32)[None, :], 0), axis=1
    )
    filled = jnp.any(matches, axis=1)
    outgoing_rows = jnp.where(
        filled[:, None], normed[source_pair // TOP], jnp.zeros((), jnp.bfloat16)
    )
    experts_here = expert_gate.shape[0]
    width = normed.shape[1]
    outgoing_rows = outgoing_rows.reshape(tensor_size, experts_here, capacity, width)
    fanned = jnp.broadcast_to(outgoing_rows[None], (group_count,) + outgoing_rows.shape)
    fanned = fanned.reshape((group_count * tensor_size,) + outgoing_rows.shape[1:])
    partial_value = run_experts(
        lax.all_to_all(fanned, ("dp", "tensor"), split_axis=0, concat_axis=0, tiled=True),
        expert_gate,
        expert_up,
        expert_down,
    ).astype(jnp.bfloat16)
    returned = lax.all_to_all(
        partial_value, ("dp", "tensor"), split_axis=0, concat_axis=0, tiled=True
    )
    slot_out = jnp.sum(
        returned.reshape(group_count, EXPERTS * capacity, width).astype(jnp.float32), axis=0
    )
    picked = slot_out[slot_of_pair].reshape(tok_rows, TOP, width)
    routed = jnp.sum(picked * route_gates[:, :, None], axis=1)
    return hidden + routed


def solution(mesh):
    return jax.shard_map(
        shards,
        mesh=mesh,
        in_specs=(
            P("dp", "tensor", None),
            P("dp", None),
            P(),
            P(),
            P("dp", "tensor", None),
            P(("dp", "tensor"), None),
            P("tensor", None),
            P(),
            P(("dp", "tensor"), None),
            P(("dp", "tensor"), None),
            P("tensor", None, "dp"),
            P("tensor", None, "dp"),
            P("tensor", "dp", None),
        ),
        out_specs=P(("dp", "tensor"), None),
        check_vma=False,
    )
```

```python
import jax
import jax.numpy as jnp
from jax import lax
from jax.sharding import PartitionSpec as P

HEADS = 16
HD = 128
EXPERTS = 64
TOP = 6
PAGE = 64


def swapped(array, axis, stride):
    return lax.ppermute(array, axis, [(i, i ^ 1 << stride) for i in range(lax.axis_size(axis))])


def local_attention(queries, cached, fresh_rows, length, cache_offset, span_offset):
    head_size = queries.shape[1]
    span_len = queries.shape[0]
    page_count = cached.shape[0]
    page_rows = cached.shape[1]
    scale_factor = 1.0 / head_size**0.5
    cache_scores = jnp.einsum(
        "qd,pjd->qpj", queries, cached[:, :, :head_size], preferred_element_type=jnp.float32
    )
    cache_scores = cache_scores.reshape(span_len, page_count * page_rows) * scale_factor
    page_ids = jnp.arange(page_count, dtype=jnp.int32)[:, None]
    row_ids = jnp.arange(page_rows, dtype=jnp.int32)[None, :]
    positions = (page_ids * PAGE + cache_offset + row_ids).reshape(-1)
    cache_scores = jnp.where(positions[None, :] < length, cache_scores, -1e30)
    new_keys = fresh_rows[:, head_size : 2 * head_size]
    new_values = fresh_rows[:, 2 * head_size :]
    span_scores = jnp.dot(queries, new_keys.T, preferred_element_type=jnp.float32) * scale_factor
    key_pos = span_offset + jnp.arange(fresh_rows.shape[0], dtype=jnp.int32)
    query_pos = jnp.arange(span_len, dtype=jnp.int32)
    span_scores = jnp.where(key_pos[None, :] <= query_pos[:, None], span_scores, -1e30)
    maximum = jnp.maximum(jnp.max(cache_scores, axis=1), jnp.max(span_scores, axis=1))
    cache_weights = jnp.exp(cache_scores - maximum[:, None])
    span_weights = jnp.exp(span_scores - maximum[:, None])
    denominator = jnp.sum(cache_weights, axis=1) + jnp.sum(span_weights, axis=1)
    rounded = cache_weights.astype(jnp.bfloat16).reshape(span_len, page_count, page_rows)
    weighted = jnp.einsum(
        "qpj,pjd->qd", rounded, cached[:, :, head_size:], preferred_element_type=jnp.float32
    )
    weighted = weighted + jnp.dot(
        span_weights.astype(jnp.bfloat16), new_values, preferred_element_type=jnp.float32
    )
    return (weighted, maximum, denominator)


def run_experts(slot_rows, expert_gate, expert_up, expert_down):
    gate_part = jnp.einsum(
        "secd,edf->secf", slot_rows, expert_gate, preferred_element_type=jnp.float32
    )
    up_part = jnp.einsum("secd,edf->secf", slot_rows, expert_up, preferred_element_type=jnp.float32)
    active = (jax.nn.silu(gate_part) * up_part).astype(jnp.bfloat16)
    return jnp.einsum("secf,efd->secd", active, expert_down, preferred_element_type=jnp.float32)


def shards(
    page_pool,
    page_table,
    destination,
    cache_len,
    new_tokens,
    residual_in,
    out_weight,
    norm_gain,
    routes,
    route_gates,
    expert_gate,
    expert_up,
    expert_down,
):
    tensor_size = lax.axis_size("tensor")
    group_count = lax.axis_size("dp")
    split_ways = max(1, tensor_size // HEADS)
    heads_here = max(1, HEADS // tensor_size)
    side_index = lax.axis_index("tensor") % split_ways
    group_index = lax.axis_index("dp")
    requests_here = page_table.shape[0]
    first_home = group_index * requests_here
    home_dest = lax.dynamic_slice_in_dim(destination, first_home, requests_here)
    dest_group = home_dest // requests_here
    group_ids = jnp.arange(group_count, dtype=jnp.int32)
    request_ids = jnp.arange(requests_here, dtype=jnp.int32)
    leaving = dest_group[None, :] == group_ids[:, None]
    chosen = jnp.sum(jnp.where(leaving, request_ids[None, :], 0), axis=1)
    chosen = jnp.where(group_ids == group_index, 0, chosen)
    outgoing = page_pool[page_table[chosen]]
    arrived = lax.all_to_all(outgoing, "dp", split_axis=0, concat_axis=0, tiled=True)
    inverse = (
        jnp.zeros_like(destination)
        .at[destination]
        .set(jnp.arange(destination.shape[0], dtype=jnp.int32))
    )
    served = lax.dynamic_slice_in_dim(inverse, first_home, requests_here)
    source = served // requests_here
    resident = source == group_index
    local_pages = page_pool[page_table[jnp.where(resident, served - first_home, 0)]]
    dense_cache = jnp.where(resident[:, None, None, None], local_pages, arrived[source])
    lengths = cache_len[served]
    fresh_per = new_tokens.shape[1] // heads_here
    span_len = fresh_per * split_ways
    rows_per_head = dense_cache.shape[2] // heads_here
    own_queries = new_tokens[:, :, :HD]
    other_queries = swapped(own_queries, "tensor", 0)
    lower_half = jnp.where(side_index == 0, own_queries, other_queries)
    upper_half = jnp.where(side_index == 0, other_queries, own_queries)
    queries = jnp.concatenate([lower_half, upper_half], axis=1)[:, None]

    def one_request(operands):
        return local_attention(
            operands[0],
            operands[1],
            operands[2],
            operands[3],
            side_index * rows_per_head,
            side_index * fresh_per,
        )

    head_results = lax.map(one_request, (queries[:, 0], dense_cache, new_tokens, lengths))
    weighted, maximum, denominator = head_results
    half_dim = HD // 2
    given_part = lax.dynamic_slice_in_dim(weighted, (1 - side_index) * half_dim, half_dim, 2)
    kept_part = lax.dynamic_slice_in_dim(weighted, side_index * half_dim, half_dim, 2)
    received_part, other_max, other_den = swapped((given_part, maximum, denominator), "tensor", 0)
    joint_max = jnp.maximum(maximum, other_max)
    own_scale = jnp.exp(maximum - joint_max)
    theirs = jnp.exp(other_max - joint_max)
    combined = kept_part * own_scale[..., None] + received_part * theirs[..., None]
    attended = combined / (denominator * own_scale + other_den * theirs)[..., None]
    tok_rows = residual_in.shape[0]
    head_out = attended.astype(jnp.bfloat16).reshape(tensor_size, tok_rows, half_dim)
    owned = lax.all_to_all(head_out, "tensor", split_axis=0, concat_axis=0, tiled=True)
    owned = owned.transpose(1, 0, 2).reshape(tok_rows, tensor_size * half_dim)
    full_weight = lax.all_gather(out_weight, "tensor", axis=0, tiled=True)
    projected = jnp.dot(owned, full_weight, preferred_element_type=jnp.float32)
    hidden = residual_in.astype(jnp.float32) + projected
    normed = (
        hidden * lax.rsqrt(jnp.mean(hidden * hidden, axis=1, keepdims=True) + 1e-06) * norm_gain
    ).astype(jnp.bfloat16)
    capacity = max(2, tok_rows * TOP * 4 // (3 * EXPERTS))
    flat_routes = routes.reshape(-1)
    pair_count = flat_routes.shape[0]
    expert_ids = jnp.arange(EXPERTS, dtype=jnp.int32)
    one_hot = (flat_routes[:, None] == expert_ids[None, :]).astype(jnp.int32)
    earlier = jnp.cumsum(one_hot, axis=0) - one_hot
    rank_in_expert = jnp.sum(earlier * one_hot, axis=1)
    slot_of_pair = flat_routes * capacity + rank_in_expert
    slot_ids = jnp.arange(EXPERTS * capacity, dtype=jnp.int32)
    matches = slot_of_pair[None, :] == slot_ids[:, None]
    source_pair = jnp.sum(
        jnp.where(matches, jnp.arange(pair_count, dtype=jnp.int32)[None, :], 0), axis=1
    )
    filled = jnp.any(matches, axis=1)
    outgoing_rows = jnp.where(
        filled[:, None], normed[source_pair // TOP], jnp.zeros((), jnp.bfloat16)
    )
    experts_here = expert_gate.shape[0]
    width = normed.shape[1]
    outgoing_rows = outgoing_rows.reshape(tensor_size, experts_here, capacity, width)
    owner_slot = (flat_routes // experts_here) * capacity + rank_in_expert
    parity = flat_routes % experts_here
    routed = jnp.zeros((tok_rows, width), jnp.float32)
    for k in range(experts_here):
        fanned = jnp.broadcast_to(outgoing_rows[None, :, k], (group_count,) + outgoing_rows[:, k].shape)
        fanned = fanned.reshape((group_count * tensor_size, capacity, width))
        arrived_rows = lax.all_to_all(fanned, ("dp", "tensor"), split_axis=0, concat_axis=0, tiled=True)
        flat_rows = arrived_rows.reshape(-1, width)
        gate_part = jnp.dot(flat_rows, expert_gate[k], preferred_element_type=jnp.float32)
        up_part = jnp.dot(flat_rows, expert_up[k], preferred_element_type=jnp.float32)
        active = (jax.nn.silu(gate_part) * up_part).astype(jnp.bfloat16)
        partial_value = jnp.dot(active, expert_down[k], preferred_element_type=jnp.float32)
        partial_value = partial_value.astype(jnp.bfloat16).reshape(arrived_rows.shape)
        returned = lax.all_to_all(
            partial_value, ("dp", "tensor"), split_axis=0, concat_axis=0, tiled=True
        )
        slot_out = jnp.sum(
            returned.reshape(group_count, tensor_size * capacity, width).astype(jnp.float32), axis=0
        )
        weight = jnp.where(parity == k, route_gates.reshape(-1), 0.0)
        picked = slot_out[owner_slot] * weight[:, None]
        routed = routed + jnp.sum(picked.reshape(tok_rows, TOP, width), axis=1)
    return hidden + routed


def solution(mesh):
    return jax.shard_map(
        shards,
        mesh=mesh,
        in_specs=(
            P("dp", "tensor", None),
            P("dp", None),
            P(),
            P(),
            P("dp", "tensor", None),
            P(("dp", "tensor"), None),
            P("tensor", None),
            P(),
            P(("dp", "tensor"), None),
            P(("dp", "tensor"), None),
            P("tensor", None, "dp"),
            P("tensor", None, "dp"),
            P("tensor", "dp", None),
        ),
        out_specs=P(("dp", "tensor"), None),
        check_vma=False,
    )
```

```python
import jax
import jax.numpy as jnp
from jax import lax
from jax.sharding import PartitionSpec as P

HEADS = 16
HD = 128
EXPERTS = 64
TOP = 6
PAGE = 64


def swapped(array, axis, stride):
    return lax.ppermute(array, axis, [(i, i ^ 1 << stride) for i in range(lax.axis_size(axis))])


def local_attention(queries, cached, fresh_rows, length, cache_offset, span_offset):
    head_size = queries.shape[1]
    span_len = queries.shape[0]
    page_count = cached.shape[0]
    page_rows = cached.shape[1]
    scale_factor = 1.0 / head_size**0.5
    cache_scores = jnp.einsum(
        "qd,pjd->qpj", queries, cached[:, :, :head_size], preferred_element_type=jnp.float32
    )
    cache_scores = cache_scores.reshape(span_len, page_count * page_rows) * scale_factor
    page_ids = jnp.arange(page_count, dtype=jnp.int32)[:, None]
    row_ids = jnp.arange(page_rows, dtype=jnp.int32)[None, :]
    positions = (page_ids * PAGE + cache_offset + row_ids).reshape(-1)
    cache_scores = jnp.where(positions[None, :] < length, cache_scores, -1e30)
    new_keys = fresh_rows[:, head_size : 2 * head_size]
    new_values = fresh_rows[:, 2 * head_size :]
    span_scores = jnp.dot(queries, new_keys.T, preferred_element_type=jnp.float32) * scale_factor
    key_pos = span_offset + jnp.arange(fresh_rows.shape[0], dtype=jnp.int32)
    query_pos = jnp.arange(span_len, dtype=jnp.int32)
    span_scores = jnp.where(key_pos[None, :] <= query_pos[:, None], span_scores, -1e30)
    maximum = jnp.maximum(jnp.max(cache_scores, axis=1), jnp.max(span_scores, axis=1))
    cache_weights = jnp.exp(cache_scores - maximum[:, None])
    span_weights = jnp.exp(span_scores - maximum[:, None])
    denominator = jnp.sum(cache_weights, axis=1) + jnp.sum(span_weights, axis=1)
    rounded = cache_weights.astype(jnp.bfloat16).reshape(span_len, page_count, page_rows)
    weighted = jnp.einsum(
        "qpj,pjd->qd", rounded, cached[:, :, head_size:], preferred_element_type=jnp.float32
    )
    weighted = weighted + jnp.dot(
        span_weights.astype(jnp.bfloat16), new_values, preferred_element_type=jnp.float32
    )
    return (weighted, maximum, denominator)


def run_experts(slot_rows, expert_gate, expert_up, expert_down):
    gate_part = jnp.einsum(
        "secd,edf->secf", slot_rows, expert_gate, preferred_element_type=jnp.float32
    )
    up_part = jnp.einsum("secd,edf->secf", slot_rows, expert_up, preferred_element_type=jnp.float32)
    active = (jax.nn.silu(gate_part) * up_part).astype(jnp.bfloat16)
    return jnp.einsum("secf,efd->secd", active, expert_down, preferred_element_type=jnp.float32)


def shards(
    page_pool,
    page_table,
    destination,
    cache_len,
    new_tokens,
    residual_in,
    out_weight,
    norm_gain,
    routes,
    route_gates,
    expert_gate,
    expert_up,
    expert_down,
):
    tensor_size = lax.axis_size("tensor")
    group_count = lax.axis_size("dp")
    split_ways = max(1, tensor_size // HEADS)
    heads_here = max(1, HEADS // tensor_size)
    side_index = lax.axis_index("tensor") % split_ways
    group_index = lax.axis_index("dp")
    requests_here = page_table.shape[0]
    first_home = group_index * requests_here
    home_dest = lax.dynamic_slice_in_dim(destination, first_home, requests_here)
    dest_group = home_dest // requests_here
    request_ids = jnp.arange(requests_here, dtype=jnp.int32)
    shifts = jnp.arange(group_count, dtype=jnp.int32)
    work_req = jnp.sum(
        jnp.where(
            dest_group[None, :] == (group_index + shifts[:, None]) % group_count,
            request_ids[None, :],
            0,
        ),
        axis=1,
    )
    inverse = (
        jnp.zeros_like(destination)
        .at[destination]
        .set(jnp.arange(destination.shape[0], dtype=jnp.int32))
    )
    served = lax.dynamic_slice_in_dim(inverse, first_home, requests_here)
    source = served // requests_here
    send_slot = jnp.sum(
        jnp.where(
            source[None, :] == (group_index - shifts[:, None]) % group_count,
            request_ids[None, :],
            0,
        ),
        axis=1,
    )
    outgoing_tokens = new_tokens[send_slot]
    fresh = [outgoing_tokens[0]]
    for j in range(1, group_count):
        fresh.append(
            lax.ppermute(
                outgoing_tokens[j], "dp", [(i, (i - j) % group_count) for i in range(group_count)]
            )
        )
    new_tokens = jnp.stack(fresh)
    dense_cache = page_pool[page_table[work_req]]
    lengths = cache_len[first_home + work_req]
    fresh_per = new_tokens.shape[1] // heads_here
    span_len = fresh_per * split_ways
    rows_per_head = dense_cache.shape[2] // heads_here
    own_queries = new_tokens[:, :, :HD]
    other_queries = swapped(own_queries, "tensor", 0)
    lower_half = jnp.where(side_index == 0, own_queries, other_queries)
    upper_half = jnp.where(side_index == 0, other_queries, own_queries)
    queries = jnp.concatenate([lower_half, upper_half], axis=1)[:, None]

    def one_request(operands):
        return local_attention(
            operands[0],
            operands[1],
            operands[2],
            operands[3],
            side_index * rows_per_head,
            side_index * fresh_per,
        )

    head_results = lax.map(one_request, (queries[:, 0], dense_cache, new_tokens, lengths))
    weighted, maximum, denominator = head_results
    half_dim = HD // 2
    given_part = lax.dynamic_slice_in_dim(weighted, (1 - side_index) * half_dim, half_dim, 2)
    kept_part = lax.dynamic_slice_in_dim(weighted, side_index * half_dim, half_dim, 2)
    received_part, other_max, other_den = swapped((given_part, maximum, denominator), "tensor", 0)
    joint_max = jnp.maximum(maximum, other_max)
    own_scale = jnp.exp(maximum - joint_max)
    theirs = jnp.exp(other_max - joint_max)
    combined = kept_part * own_scale[..., None] + received_part * theirs[..., None]
    attended = combined / (denominator * own_scale + other_den * theirs)[..., None]
    attended = attended.astype(jnp.bfloat16)
    back = [attended[0]]
    for j in range(1, group_count):
        back.append(
            lax.ppermute(attended[j], "dp", [(i, (i + j) % group_count) for i in range(group_count)])
        )
    attended = jnp.stack(back)[(group_index - source) % group_count]
    tok_rows = residual_in.shape[0]
    head_out = attended.reshape(tensor_size, tok_rows, half_dim)
    owned = lax.all_to_all(head_out, "tensor", split_axis=0, concat_axis=0, tiled=True)
    owned = owned.transpose(1, 0, 2).reshape(tok_rows, tensor_size * half_dim)
    full_weight = lax.all_gather(out_weight, "tensor", axis=0, tiled=True)
    projected = jnp.dot(owned, full_weight, preferred_element_type=jnp.float32)
    hidden = residual_in.astype(jnp.float32) + projected
    normed = (
        hidden * lax.rsqrt(jnp.mean(hidden * hidden, axis=1, keepdims=True) + 1e-06) * norm_gain
    ).astype(jnp.bfloat16)
    capacity = max(2, tok_rows * TOP * 4 // (3 * EXPERTS))
    flat_routes = routes.reshape(-1)
    pair_count = flat_routes.shape[0]
    expert_ids = jnp.arange(EXPERTS, dtype=jnp.int32)
    one_hot = (flat_routes[:, None] == expert_ids[None, :]).astype(jnp.int32)
    earlier = jnp.cumsum(one_hot, axis=0) - one_hot
    rank_in_expert = jnp.sum(earlier * one_hot, axis=1)
    slot_of_pair = flat_routes * capacity + rank_in_expert
    slot_ids = jnp.arange(EXPERTS * capacity, dtype=jnp.int32)
    matches = slot_of_pair[None, :] == slot_ids[:, None]
    source_pair = jnp.sum(
        jnp.where(matches, jnp.arange(pair_count, dtype=jnp.int32)[None, :], 0), axis=1
    )
    filled = jnp.any(matches, axis=1)
    outgoing_rows = jnp.where(
        filled[:, None], normed[source_pair // TOP], jnp.zeros((), jnp.bfloat16)
    )
    experts_here = expert_gate.shape[0]
    width = normed.shape[1]
    outgoing_rows = outgoing_rows.reshape(tensor_size, experts_here, capacity, width)
    owner_slot = (flat_routes // experts_here) * capacity + rank_in_expert
    parity = flat_routes % experts_here
    routed = jnp.zeros((tok_rows, width), jnp.float32)
    for k in range(experts_here):
        fanned = jnp.broadcast_to(outgoing_rows[None, :, k], (group_count,) + outgoing_rows[:, k].shape)
        fanned = fanned.reshape((group_count * tensor_size, capacity, width))
        arrived_rows = lax.all_to_all(fanned, ("dp", "tensor"), split_axis=0, concat_axis=0, tiled=True)
        flat_rows = arrived_rows.reshape(-1, width)
        gate_part = jnp.dot(flat_rows, expert_gate[k], preferred_element_type=jnp.float32)
        up_part = jnp.dot(flat_rows, expert_up[k], preferred_element_type=jnp.float32)
        active = (jax.nn.silu(gate_part) * up_part).astype(jnp.bfloat16)
        partial_value = jnp.dot(active, expert_down[k], preferred_element_type=jnp.float32)
        partial_value = partial_value.astype(jnp.bfloat16).reshape(arrived_rows.shape)
        returned = lax.all_to_all(
            partial_value, ("dp", "tensor"), split_axis=0, concat_axis=0, tiled=True
        )
        slot_out = jnp.sum(
            returned.reshape(group_count, tensor_size * capacity, width).astype(jnp.float32), axis=0
        )
        weight = jnp.where(parity == k, route_gates.reshape(-1), 0.0)
        picked = slot_out[owner_slot] * weight[:, None]
        routed = routed + jnp.sum(picked.reshape(tok_rows, TOP, width), axis=1)
    return hidden + routed


def solution(mesh):
    return jax.shard_map(
        shards,
        mesh=mesh,
        in_specs=(
            P("dp", "tensor", None),
            P("dp", None),
            P(),
            P(),
            P("dp", "tensor", None),
            P(("dp", "tensor"), None),
            P("tensor", None),
            P(),
            P(("dp", "tensor"), None),
            P(("dp", "tensor"), None),
            P("tensor", None, "dp"),
            P("tensor", None, "dp"),
            P("tensor", "dp", None),
        ),
        out_specs=P(("dp", "tensor"), None),
        check_vma=False,
    )
```

```python
import functools

import jax
import jax.numpy as jnp
from jax import lax
from jax.experimental import pallas as pl
from jax.experimental.pallas import tpu as pltpu
from jax.sharding import PartitionSpec as P

HEADS = 16
HD = 128
EXPERTS = 64
TOP = 6
PAGE = 64


def swapped(array, axis, stride):
    return lax.ppermute(array, axis, [(i, i ^ 1 << stride) for i in range(lax.axis_size(axis))])


def attn_body(scal_ref, q_ref, c_ref, f_ref, w_ref, m_ref, d_ref, *, block_q, page_rows, head):
    item = pl.program_id(0)
    qb = pl.program_id(1)
    length = scal_ref[item]
    cache_offset = scal_ref[4]
    span_offset = scal_ref[5]
    scale = 1.0 / head**0.5
    q = q_ref[...]
    cached = c_ref[...]
    fresh = f_ref[...]
    dims = (((1,), (1,)), ((), ()))
    cs = lax.dot_general(q, cached[:, :head], dims, preferred_element_type=jnp.float32) * scale
    n = lax.broadcasted_iota(jnp.int32, cs.shape, 1)
    pos = (n // page_rows) * PAGE + cache_offset + n % page_rows
    cs = jnp.where(pos < length, cs, -1e30)
    ss = lax.dot_general(q, fresh[:, head:2 * head], dims, preferred_element_type=jnp.float32) * scale
    kpos = span_offset + lax.broadcasted_iota(jnp.int32, ss.shape, 1)
    qpos = qb * block_q + lax.broadcasted_iota(jnp.int32, ss.shape, 0)
    ss = jnp.where(kpos <= qpos, ss, -1e30)
    mx = jnp.maximum(jnp.max(cs, axis=1, keepdims=True), jnp.max(ss, axis=1, keepdims=True))
    cw = jnp.exp(cs - mx)
    sw = jnp.exp(ss - mx)
    den = jnp.sum(cw, axis=1, keepdims=True) + jnp.sum(sw, axis=1, keepdims=True)
    acc = jnp.dot(cw.astype(jnp.bfloat16), cached[:, head:], preferred_element_type=jnp.float32)
    acc = acc + jnp.dot(sw.astype(jnp.bfloat16), fresh[:, 2 * head:], preferred_element_type=jnp.float32)
    w_ref[...] = acc
    m_ref[...] = mx
    d_ref[...] = den


def attention_kernel(queries, cached, fresh, lengths, cache_offset, span_offset, interpret=False):
    items, span, head = queries.shape
    pages, page_rows = cached.shape[1], cached.shape[2]
    keys = pages * page_rows
    cached = cached.reshape(items, keys, cached.shape[3])
    fresh_rows = fresh.shape[1]
    block_q = 256
    scal = jnp.concatenate(
        [lengths.astype(jnp.int32), jnp.stack([cache_offset, span_offset]).astype(jnp.int32)]
    )
    body = functools.partial(attn_body, block_q=block_q, page_rows=page_rows, head=head)
    grid_spec = pltpu.PrefetchScalarGridSpec(
        num_scalar_prefetch=1,
        grid=(items, span // block_q),
        in_specs=[
            pl.BlockSpec((None, block_q, head), lambda i, b, s: (i, b, 0)),
            pl.BlockSpec((None, keys, 2 * head), lambda i, b, s: (i, 0, 0)),
            pl.BlockSpec((None, fresh_rows, 3 * head), lambda i, b, s: (i, 0, 0)),
        ],
        out_specs=[
            pl.BlockSpec((None, block_q, head), lambda i, b, s: (i, b, 0)),
            pl.BlockSpec((None, block_q, 1), lambda i, b, s: (i, b, 0)),
            pl.BlockSpec((None, block_q, 1), lambda i, b, s: (i, b, 0)),
        ],
    )
    weighted, mx, den = pl.pallas_call(
        body,
        grid_spec=grid_spec,
        out_shape=[
            jax.ShapeDtypeStruct((items, span, head), jnp.float32),
            jax.ShapeDtypeStruct((items, span, 1), jnp.float32),
            jax.ShapeDtypeStruct((items, span, 1), jnp.float32),
        ],
        interpret=interpret,
    )(scal, queries, cached, fresh)
    return weighted, mx[..., 0], den[..., 0]


def run_experts(slot_rows, expert_gate, expert_up, expert_down):
    gate_part = jnp.einsum(
        "secd,edf->secf", slot_rows, expert_gate, preferred_element_type=jnp.float32
    )
    up_part = jnp.einsum("secd,edf->secf", slot_rows, expert_up, preferred_element_type=jnp.float32)
    active = (jax.nn.silu(gate_part) * up_part).astype(jnp.bfloat16)
    return jnp.einsum("secf,efd->secd", active, expert_down, preferred_element_type=jnp.float32)


def shards(
    page_pool,
    page_table,
    destination,
    cache_len,
    new_tokens,
    residual_in,
    out_weight,
    norm_gain,
    routes,
    route_gates,
    expert_gate,
    expert_up,
    expert_down,
):
    tensor_size = lax.axis_size("tensor")
    group_count = lax.axis_size("dp")
    split_ways = max(1, tensor_size // HEADS)
    heads_here = max(1, HEADS // tensor_size)
    side_index = lax.axis_index("tensor") % split_ways
    group_index = lax.axis_index("dp")
    requests_here = page_table.shape[0]
    first_home = group_index * requests_here
    home_dest = lax.dynamic_slice_in_dim(destination, first_home, requests_here)
    dest_group = home_dest // requests_here
    request_ids = jnp.arange(requests_here, dtype=jnp.int32)
    shifts = jnp.arange(group_count, dtype=jnp.int32)
    work_req = jnp.sum(
        jnp.where(
            dest_group[None, :] == (group_index + shifts[:, None]) % group_count,
            request_ids[None, :],
            0,
        ),
        axis=1,
    )
    inverse = (
        jnp.zeros_like(destination)
        .at[destination]
        .set(jnp.arange(destination.shape[0], dtype=jnp.int32))
    )
    served = lax.dynamic_slice_in_dim(inverse, first_home, requests_here)
    source = served // requests_here
    send_slot = jnp.sum(
        jnp.where(
            source[None, :] == (group_index - shifts[:, None]) % group_count,
            request_ids[None, :],
            0,
        ),
        axis=1,
    )
    outgoing_tokens = new_tokens[send_slot]
    fresh = [outgoing_tokens[0]]
    for j in range(1, group_count):
        fresh.append(
            lax.ppermute(
                outgoing_tokens[j], "dp", [(i, (i - j) % group_count) for i in range(group_count)]
            )
        )
    new_tokens = jnp.stack(fresh)
    dense_cache = page_pool[page_table[work_req]]
    lengths = cache_len[first_home + work_req]
    fresh_per = new_tokens.shape[1] // heads_here
    span_len = fresh_per * split_ways
    rows_per_head = dense_cache.shape[2] // heads_here
    own_queries = new_tokens[:, :, :HD]
    other_queries = swapped(own_queries, "tensor", 0)
    lower_half = jnp.where(side_index == 0, own_queries, other_queries)
    upper_half = jnp.where(side_index == 0, other_queries, own_queries)
    queries = jnp.concatenate([lower_half, upper_half], axis=1)[:, None]

    head_results = attention_kernel(
        queries[:, 0],
        dense_cache,
        new_tokens,
        lengths,
        side_index * rows_per_head,
        side_index * fresh_per,
    )
    weighted, maximum, denominator = head_results
    half_dim = HD // 2
    given_part = lax.dynamic_slice_in_dim(weighted, (1 - side_index) * half_dim, half_dim, 2)
    kept_part = lax.dynamic_slice_in_dim(weighted, side_index * half_dim, half_dim, 2)
    received_part, other_max, other_den = swapped((given_part, maximum, denominator), "tensor", 0)
    joint_max = jnp.maximum(maximum, other_max)
    own_scale = jnp.exp(maximum - joint_max)
    theirs = jnp.exp(other_max - joint_max)
    combined = kept_part * own_scale[..., None] + received_part * theirs[..., None]
    attended = combined / (denominator * own_scale + other_den * theirs)[..., None]
    attended = attended.astype(jnp.bfloat16)
    back = [attended[0]]
    for j in range(1, group_count):
        back.append(
            lax.ppermute(attended[j], "dp", [(i, (i + j) % group_count) for i in range(group_count)])
        )
    attended = jnp.stack(back)[(group_index - source) % group_count]
    tok_rows = residual_in.shape[0]
    head_out = attended.reshape(tensor_size, tok_rows, half_dim)
    owned = lax.all_to_all(head_out, "tensor", split_axis=0, concat_axis=0, tiled=True)
    owned = owned.transpose(1, 0, 2).reshape(tok_rows, tensor_size * half_dim)
    full_weight = lax.all_gather(out_weight, "tensor", axis=0, tiled=True)
    projected = jnp.dot(owned, full_weight, preferred_element_type=jnp.float32)
    hidden = residual_in.astype(jnp.float32) + projected
    normed = (
        hidden * lax.rsqrt(jnp.mean(hidden * hidden, axis=1, keepdims=True) + 1e-06) * norm_gain
    ).astype(jnp.bfloat16)
    capacity = max(2, tok_rows * TOP * 4 // (3 * EXPERTS))
    flat_routes = routes.reshape(-1)
    pair_count = flat_routes.shape[0]
    expert_ids = jnp.arange(EXPERTS, dtype=jnp.int32)
    one_hot = (flat_routes[:, None] == expert_ids[None, :]).astype(jnp.int32)
    earlier = jnp.cumsum(one_hot, axis=0) - one_hot
    rank_in_expert = jnp.sum(earlier * one_hot, axis=1)
    slot_of_pair = flat_routes * capacity + rank_in_expert
    slot_ids = jnp.arange(EXPERTS * capacity, dtype=jnp.int32)
    matches = slot_of_pair[None, :] == slot_ids[:, None]
    source_pair = jnp.sum(
        jnp.where(matches, jnp.arange(pair_count, dtype=jnp.int32)[None, :], 0), axis=1
    )
    filled = jnp.any(matches, axis=1)
    outgoing_rows = jnp.where(
        filled[:, None], normed[source_pair // TOP], jnp.zeros((), jnp.bfloat16)
    )
    experts_here = expert_gate.shape[0]
    width = normed.shape[1]
    outgoing_rows = outgoing_rows.reshape(tensor_size, experts_here, capacity, width)
    owner_slot = (flat_routes // experts_here) * capacity + rank_in_expert
    parity = flat_routes % experts_here
    routed = jnp.zeros((tok_rows, width), jnp.float32)
    for k in range(experts_here):
        fanned = jnp.broadcast_to(outgoing_rows[None, :, k], (group_count,) + outgoing_rows[:, k].shape)
        fanned = fanned.reshape((group_count * tensor_size, capacity, width))
        arrived_rows = lax.all_to_all(fanned, ("dp", "tensor"), split_axis=0, concat_axis=0, tiled=True)
        flat_rows = arrived_rows.reshape(-1, width)
        gate_part = jnp.dot(flat_rows, expert_gate[k], preferred_element_type=jnp.float32)
        up_part = jnp.dot(flat_rows, expert_up[k], preferred_element_type=jnp.float32)
        active = (jax.nn.silu(gate_part) * up_part).astype(jnp.bfloat16)
        partial_value = jnp.dot(active, expert_down[k], preferred_element_type=jnp.float32)
        partial_value = partial_value.astype(jnp.bfloat16).reshape(arrived_rows.shape)
        returned = lax.all_to_all(
            partial_value, ("dp", "tensor"), split_axis=0, concat_axis=0, tiled=True
        )
        slot_out = jnp.sum(
            returned.reshape(group_count, tensor_size * capacity, width).astype(jnp.float32), axis=0
        )
        weight = jnp.where(parity == k, route_gates.reshape(-1), 0.0)
        picked = slot_out[owner_slot] * weight[:, None]
        routed = routed + jnp.sum(picked.reshape(tok_rows, TOP, width), axis=1)
    return hidden + routed


def solution(mesh):
    return jax.shard_map(
        shards,
        mesh=mesh,
        in_specs=(
            P("dp", "tensor", None),
            P("dp", None),
            P(),
            P(),
            P("dp", "tensor", None),
            P(("dp", "tensor"), None),
            P("tensor", None),
            P(),
            P(("dp", "tensor"), None),
            P(("dp", "tensor"), None),
            P("tensor", None, "dp"),
            P("tensor", None, "dp"),
            P("tensor", "dp", None),
        ),
        out_specs=P(("dp", "tensor"), None),
        check_vma=False,
    )
```

```python
import functools

import jax
import jax.numpy as jnp
from jax import lax
from jax.experimental import pallas as pl
from jax.experimental.pallas import tpu as pltpu
from jax.sharding import PartitionSpec as P

HEADS = 16
HD = 128
EXPERTS = 64
TOP = 6
PAGE = 64


def swapped(array, axis, stride):
    return lax.ppermute(array, axis, [(i, i ^ 1 << stride) for i in range(lax.axis_size(axis))])


def attn_body(scal_ref, q_ref, c_ref, f_ref, w_ref, m_ref, d_ref, *, block_q, page_rows, head):
    item = pl.program_id(0)
    qb = pl.program_id(1)
    length = scal_ref[item]
    cache_offset = scal_ref[4]
    span_offset = scal_ref[5]
    scale = 1.0 / head**0.5
    q = q_ref[...]
    cached = c_ref[...]
    fresh = f_ref[...]
    dims = (((1,), (1,)), ((), ()))
    cs = lax.dot_general(q, cached[:, :head], dims, preferred_element_type=jnp.float32) * scale
    n = lax.broadcasted_iota(jnp.int32, cs.shape, 1)
    pos = (n // page_rows) * PAGE + cache_offset + n % page_rows
    cs = jnp.where(pos < length, cs, -1e30)
    ss = lax.dot_general(q, fresh[:, head:2 * head], dims, preferred_element_type=jnp.float32) * scale
    kpos = span_offset + lax.broadcasted_iota(jnp.int32, ss.shape, 1)
    qpos = qb * block_q + lax.broadcasted_iota(jnp.int32, ss.shape, 0)
    ss = jnp.where(kpos <= qpos, ss, -1e30)
    mx = jnp.maximum(jnp.max(cs, axis=1, keepdims=True), jnp.max(ss, axis=1, keepdims=True))
    cw = jnp.exp(cs - mx)
    sw = jnp.exp(ss - mx)
    den = jnp.sum(cw, axis=1, keepdims=True) + jnp.sum(sw, axis=1, keepdims=True)
    acc = jnp.dot(cw.astype(jnp.bfloat16), cached[:, head:], preferred_element_type=jnp.float32)
    acc = acc + jnp.dot(sw.astype(jnp.bfloat16), fresh[:, 2 * head:], preferred_element_type=jnp.float32)
    w_ref[...] = acc
    m_ref[...] = mx
    d_ref[...] = den


def attention_kernel(queries, cached, fresh, lengths, cache_offset, span_offset, interpret=False):
    items, span, head = queries.shape
    pages, page_rows = cached.shape[1], cached.shape[2]
    keys = pages * page_rows
    cached = cached.reshape(items, keys, cached.shape[3])
    fresh_rows = fresh.shape[1]
    block_q = 256
    scal = jnp.concatenate(
        [lengths.astype(jnp.int32), jnp.stack([cache_offset, span_offset]).astype(jnp.int32)]
    )
    body = functools.partial(attn_body, block_q=block_q, page_rows=page_rows, head=head)
    grid_spec = pltpu.PrefetchScalarGridSpec(
        num_scalar_prefetch=1,
        grid=(items, span // block_q),
        in_specs=[
            pl.BlockSpec((None, block_q, head), lambda i, b, s: (i, b, 0)),
            pl.BlockSpec((None, keys, 2 * head), lambda i, b, s: (i, 0, 0)),
            pl.BlockSpec((None, fresh_rows, 3 * head), lambda i, b, s: (i, 0, 0)),
        ],
        out_specs=[
            pl.BlockSpec((None, block_q, head), lambda i, b, s: (i, b, 0)),
            pl.BlockSpec((None, block_q, 1), lambda i, b, s: (i, b, 0)),
            pl.BlockSpec((None, block_q, 1), lambda i, b, s: (i, b, 0)),
        ],
    )
    weighted, mx, den = pl.pallas_call(
        body,
        grid_spec=grid_spec,
        out_shape=[
            jax.ShapeDtypeStruct((items, span, head), jnp.float32),
            jax.ShapeDtypeStruct((items, span, 1), jnp.float32),
            jax.ShapeDtypeStruct((items, span, 1), jnp.float32),
        ],
        interpret=interpret,
    )(scal, queries, cached, fresh)
    return weighted, mx[..., 0], den[..., 0]


def run_experts(slot_rows, expert_gate, expert_up, expert_down):
    gate_part = jnp.einsum(
        "secd,edf->secf", slot_rows, expert_gate, preferred_element_type=jnp.float32
    )
    up_part = jnp.einsum("secd,edf->secf", slot_rows, expert_up, preferred_element_type=jnp.float32)
    active = (jax.nn.silu(gate_part) * up_part).astype(jnp.bfloat16)
    return jnp.einsum("secf,efd->secd", active, expert_down, preferred_element_type=jnp.float32)


def shards(
    page_pool,
    page_table,
    destination,
    cache_len,
    new_tokens,
    residual_in,
    out_weight,
    norm_gain,
    routes,
    route_gates,
    expert_gate,
    expert_up,
    expert_down,
):
    tensor_size = lax.axis_size("tensor")
    group_count = lax.axis_size("dp")
    split_ways = max(1, tensor_size // HEADS)
    heads_here = max(1, HEADS // tensor_size)
    side_index = lax.axis_index("tensor") % split_ways
    group_index = lax.axis_index("dp")
    requests_here = page_table.shape[0]
    first_home = group_index * requests_here
    home_dest = lax.dynamic_slice_in_dim(destination, first_home, requests_here)
    dest_group = home_dest // requests_here
    request_ids = jnp.arange(requests_here, dtype=jnp.int32)
    shifts = jnp.arange(group_count, dtype=jnp.int32)
    work_req = jnp.sum(
        jnp.where(
            dest_group[None, :] == (group_index + shifts[:, None]) % group_count,
            request_ids[None, :],
            0,
        ),
        axis=1,
    )
    inverse = (
        jnp.zeros_like(destination)
        .at[destination]
        .set(jnp.arange(destination.shape[0], dtype=jnp.int32))
    )
    served = lax.dynamic_slice_in_dim(inverse, first_home, requests_here)
    source = served // requests_here
    send_slot = jnp.sum(
        jnp.where(
            source[None, :] == (group_index - shifts[:, None]) % group_count,
            request_ids[None, :],
            0,
        ),
        axis=1,
    )
    outgoing_tokens = new_tokens[send_slot]
    fresh = [outgoing_tokens[0]]
    for j in range(1, group_count):
        fresh.append(
            lax.ppermute(
                outgoing_tokens[j], "dp", [(i, (i - j) % group_count) for i in range(group_count)]
            )
        )
    new_tokens = jnp.stack(fresh)
    dense_cache = page_pool[page_table[work_req]]
    lengths = cache_len[first_home + work_req]
    fresh_per = new_tokens.shape[1] // heads_here
    span_len = fresh_per * split_ways
    rows_per_head = dense_cache.shape[2] // heads_here
    own_queries = new_tokens[:, :, :HD]
    other_queries = swapped(own_queries, "tensor", 0)
    lower_half = jnp.where(side_index == 0, own_queries, other_queries)
    upper_half = jnp.where(side_index == 0, other_queries, own_queries)
    queries = jnp.concatenate([lower_half, upper_half], axis=1)[:, None]

    head_results = attention_kernel(
        queries[:, 0],
        dense_cache,
        new_tokens,
        lengths,
        side_index * rows_per_head,
        side_index * fresh_per,
    )
    weighted, maximum, denominator = head_results
    half_dim = HD // 2
    given_part = lax.dynamic_slice_in_dim(weighted, (1 - side_index) * half_dim, half_dim, 2)
    kept_part = lax.dynamic_slice_in_dim(weighted, side_index * half_dim, half_dim, 2)
    received_part, other_max, other_den = swapped((given_part, maximum, denominator), "tensor", 0)
    joint_max = jnp.maximum(maximum, other_max)
    own_scale = jnp.exp(maximum - joint_max)
    theirs = jnp.exp(other_max - joint_max)
    combined = kept_part * own_scale[..., None] + received_part * theirs[..., None]
    attended = combined / (denominator * own_scale + other_den * theirs)[..., None]
    attended = attended.astype(jnp.bfloat16)
    tok_rows = residual_in.shape[0]
    chunks = span_len // tok_rows
    by_dest = attended[(shifts - group_index) % group_count]
    by_dest = by_dest.reshape(group_count, 1, chunks, tok_rows, half_dim)
    send = jnp.broadcast_to(by_dest, (group_count, requests_here, chunks, tok_rows, half_dim))
    send = send.reshape(group_count * tensor_size, tok_rows, half_dim)
    received = lax.all_to_all(send, ("dp", "tensor"), split_axis=0, concat_axis=0, tiled=True)
    received = received.reshape(group_count, tensor_size, tok_rows, half_dim)
    home_of_slot = source[lax.axis_index("tensor") // chunks]
    owned = lax.dynamic_index_in_dim(received, home_of_slot, 0, keepdims=False)
    owned = owned.transpose(1, 0, 2).reshape(tok_rows, tensor_size * half_dim)
    full_weight = lax.all_gather(out_weight, "tensor", axis=0, tiled=True)
    projected = jnp.dot(owned, full_weight, preferred_element_type=jnp.float32)
    hidden = residual_in.astype(jnp.float32) + projected
    normed = (
        hidden * lax.rsqrt(jnp.mean(hidden * hidden, axis=1, keepdims=True) + 1e-06) * norm_gain
    ).astype(jnp.bfloat16)
    capacity = max(2, tok_rows * TOP * 4 // (3 * EXPERTS))
    flat_routes = routes.reshape(-1)
    pair_count = flat_routes.shape[0]
    expert_ids = jnp.arange(EXPERTS, dtype=jnp.int32)
    one_hot = (flat_routes[:, None] == expert_ids[None, :]).astype(jnp.int32)
    earlier = jnp.cumsum(one_hot, axis=0) - one_hot
    rank_in_expert = jnp.sum(earlier * one_hot, axis=1)
    slot_of_pair = flat_routes * capacity + rank_in_expert
    slot_ids = jnp.arange(EXPERTS * capacity, dtype=jnp.int32)
    matches = slot_of_pair[None, :] == slot_ids[:, None]
    source_pair = jnp.sum(
        jnp.where(matches, jnp.arange(pair_count, dtype=jnp.int32)[None, :], 0), axis=1
    )
    filled = jnp.any(matches, axis=1)
    outgoing_rows = jnp.where(
        filled[:, None], normed[source_pair // TOP], jnp.zeros((), jnp.bfloat16)
    )
    experts_here = expert_gate.shape[0]
    width = normed.shape[1]
    outgoing_rows = outgoing_rows.reshape(tensor_size, experts_here, capacity, width)
    owner_slot = (flat_routes // experts_here) * capacity + rank_in_expert
    parity = flat_routes % experts_here
    routed = jnp.zeros((tok_rows, width), jnp.float32)
    for k in range(experts_here):
        fanned = jnp.broadcast_to(outgoing_rows[None, :, k], (group_count,) + outgoing_rows[:, k].shape)
        fanned = fanned.reshape((group_count * tensor_size, capacity, width))
        arrived_rows = lax.all_to_all(fanned, ("dp", "tensor"), split_axis=0, concat_axis=0, tiled=True)
        flat_rows = arrived_rows.reshape(-1, width)
        gate_part = jnp.dot(flat_rows, expert_gate[k], preferred_element_type=jnp.float32)
        up_part = jnp.dot(flat_rows, expert_up[k], preferred_element_type=jnp.float32)
        active = (jax.nn.silu(gate_part) * up_part).astype(jnp.bfloat16)
        partial_value = jnp.dot(active, expert_down[k], preferred_element_type=jnp.float32)
        partial_value = partial_value.astype(jnp.bfloat16).reshape(arrived_rows.shape)
        returned = lax.all_to_all(
            partial_value, ("dp", "tensor"), split_axis=0, concat_axis=0, tiled=True
        )
        slot_out = jnp.sum(
            returned.reshape(group_count, tensor_size * capacity, width).astype(jnp.float32), axis=0
        )
        weight = jnp.where(parity == k, route_gates.reshape(-1), 0.0)
        picked = slot_out[owner_slot] * weight[:, None]
        routed = routed + jnp.sum(picked.reshape(tok_rows, TOP, width), axis=1)
    return hidden + routed


def solution(mesh):
    return jax.shard_map(
        shards,
        mesh=mesh,
        in_specs=(
            P("dp", "tensor", None),
            P("dp", None),
            P(),
            P(),
            P("dp", "tensor", None),
            P(("dp", "tensor"), None),
            P("tensor", None),
            P(),
            P(("dp", "tensor"), None),
            P(("dp", "tensor"), None),
            P("tensor", None, "dp"),
            P("tensor", None, "dp"),
            P("tensor", "dp", None),
        ),
        out_specs=P(("dp", "tensor"), None),
        check_vma=False,
    )
```

```python
import functools

import jax
import jax.numpy as jnp
from jax import lax
from jax.experimental import pallas as pl
from jax.experimental.pallas import tpu as pltpu
from jax.sharding import PartitionSpec as P

HEADS = 16
HD = 128
EXPERTS = 64
TOP = 6
PAGE = 64


def swapped(array, axis, stride):
    return lax.ppermute(array, axis, [(i, i ^ 1 << stride) for i in range(lax.axis_size(axis))])


def attn_body(scal_ref, q_ref, c_ref, f_ref, w_ref, m_ref, d_ref, *, block_q, page_rows, head):
    item = pl.program_id(0)
    qb = pl.program_id(1)
    length = scal_ref[item]
    cache_offset = scal_ref[4]
    span_offset = scal_ref[5]
    scale = 1.0 / head**0.5
    q = q_ref[...]
    cached = c_ref[...]
    fresh = f_ref[...]
    dims = (((1,), (1,)), ((), ()))
    cs = lax.dot_general(q, cached[:, :head], dims, preferred_element_type=jnp.float32) * scale
    n = lax.broadcasted_iota(jnp.int32, cs.shape, 1)
    pos = (n // page_rows) * PAGE + cache_offset + n % page_rows
    cs = jnp.where(pos < length, cs, -1e30)
    ss = lax.dot_general(q, fresh[:, head:2 * head], dims, preferred_element_type=jnp.float32) * scale
    kpos = span_offset + lax.broadcasted_iota(jnp.int32, ss.shape, 1)
    qpos = qb * block_q + lax.broadcasted_iota(jnp.int32, ss.shape, 0)
    ss = jnp.where(kpos <= qpos, ss, -1e30)
    mx = jnp.maximum(jnp.max(cs, axis=1, keepdims=True), jnp.max(ss, axis=1, keepdims=True))
    cw = jnp.exp(cs - mx)
    sw = jnp.exp(ss - mx)
    den = jnp.sum(cw, axis=1, keepdims=True) + jnp.sum(sw, axis=1, keepdims=True)
    acc = jnp.dot(cw.astype(jnp.bfloat16), cached[:, head:], preferred_element_type=jnp.float32)
    acc = acc + jnp.dot(sw.astype(jnp.bfloat16), fresh[:, 2 * head:], preferred_element_type=jnp.float32)
    w_ref[...] = acc
    m_ref[...] = mx
    d_ref[...] = den


def attention_kernel(queries, cached, fresh, lengths, cache_offset, span_offset, interpret=False):
    items, span, head = queries.shape
    pages, page_rows = cached.shape[1], cached.shape[2]
    keys = pages * page_rows
    cached = cached.reshape(items, keys, cached.shape[3])
    fresh_rows = fresh.shape[1]
    block_q = 256
    scal = jnp.concatenate(
        [lengths.astype(jnp.int32), jnp.stack([cache_offset, span_offset]).astype(jnp.int32)]
    )
    body = functools.partial(attn_body, block_q=block_q, page_rows=page_rows, head=head)
    grid_spec = pltpu.PrefetchScalarGridSpec(
        num_scalar_prefetch=1,
        grid=(items, span // block_q),
        in_specs=[
            pl.BlockSpec((None, block_q, head), lambda i, b, s: (i, b, 0)),
            pl.BlockSpec((None, keys, 2 * head), lambda i, b, s: (i, 0, 0)),
            pl.BlockSpec((None, fresh_rows, 3 * head), lambda i, b, s: (i, 0, 0)),
        ],
        out_specs=[
            pl.BlockSpec((None, block_q, head), lambda i, b, s: (i, b, 0)),
            pl.BlockSpec((None, block_q, 1), lambda i, b, s: (i, b, 0)),
            pl.BlockSpec((None, block_q, 1), lambda i, b, s: (i, b, 0)),
        ],
    )
    weighted, mx, den = pl.pallas_call(
        body,
        grid_spec=grid_spec,
        out_shape=[
            jax.ShapeDtypeStruct((items, span, head), jnp.float32),
            jax.ShapeDtypeStruct((items, span, 1), jnp.float32),
            jax.ShapeDtypeStruct((items, span, 1), jnp.float32),
        ],
        interpret=interpret,
    )(scal, queries, cached, fresh)
    return weighted, mx[..., 0], den[..., 0]


def run_experts(slot_rows, expert_gate, expert_up, expert_down):
    gate_part = jnp.einsum(
        "secd,edf->secf", slot_rows, expert_gate, preferred_element_type=jnp.float32
    )
    up_part = jnp.einsum("secd,edf->secf", slot_rows, expert_up, preferred_element_type=jnp.float32)
    active = (jax.nn.silu(gate_part) * up_part).astype(jnp.bfloat16)
    return jnp.einsum("secf,efd->secd", active, expert_down, preferred_element_type=jnp.float32)


def shards(
    page_pool,
    page_table,
    destination,
    cache_len,
    new_tokens,
    residual_in,
    out_weight,
    norm_gain,
    routes,
    route_gates,
    expert_gate,
    expert_up,
    expert_down,
):
    tensor_size = lax.axis_size("tensor")
    group_count = lax.axis_size("dp")
    split_ways = max(1, tensor_size // HEADS)
    heads_here = max(1, HEADS // tensor_size)
    side_index = lax.axis_index("tensor") % split_ways
    group_index = lax.axis_index("dp")
    requests_here = page_table.shape[0]
    first_home = group_index * requests_here
    home_dest = lax.dynamic_slice_in_dim(destination, first_home, requests_here)
    dest_group = home_dest // requests_here
    request_ids = jnp.arange(requests_here, dtype=jnp.int32)
    shifts = jnp.arange(group_count, dtype=jnp.int32)
    work_req = jnp.sum(
        jnp.where(
            dest_group[None, :] == (group_index + shifts[:, None]) % group_count,
            request_ids[None, :],
            0,
        ),
        axis=1,
    )
    inverse = (
        jnp.zeros_like(destination)
        .at[destination]
        .set(jnp.arange(destination.shape[0], dtype=jnp.int32))
    )
    served = lax.dynamic_slice_in_dim(inverse, first_home, requests_here)
    source = served // requests_here
    send_slot = jnp.sum(
        jnp.where(
            source[None, :] == (group_index - shifts[:, None]) % group_count,
            request_ids[None, :],
            0,
        ),
        axis=1,
    )
    outgoing_tokens = new_tokens[send_slot]
    fresh = [outgoing_tokens[0]]
    for j in range(1, group_count):
        fresh.append(
            lax.ppermute(
                outgoing_tokens[j], "dp", [(i, (i - j) % group_count) for i in range(group_count)]
            )
        )
    new_tokens = jnp.stack(fresh)
    dense_cache = page_pool[page_table[work_req]]
    lengths = cache_len[first_home + work_req]
    fresh_per = new_tokens.shape[1] // heads_here
    span_len = fresh_per * split_ways
    rows_per_head = dense_cache.shape[2] // heads_here
    own_queries = new_tokens[:, :, :HD]
    other_queries = swapped(own_queries, "tensor", 0)
    lower_half = jnp.where(side_index == 0, own_queries, other_queries)
    upper_half = jnp.where(side_index == 0, other_queries, own_queries)
    queries = jnp.concatenate([lower_half, upper_half], axis=1)[:, None]

    head_results = attention_kernel(
        queries[:, 0],
        dense_cache,
        new_tokens,
        lengths,
        side_index * rows_per_head,
        side_index * fresh_per,
    )
    weighted, maximum, denominator = head_results
    half_dim = HD // 2
    given_part = lax.dynamic_slice_in_dim(weighted, (1 - side_index) * half_dim, half_dim, 2)
    kept_part = lax.dynamic_slice_in_dim(weighted, side_index * half_dim, half_dim, 2)
    received_part, other_max, other_den = swapped((given_part, maximum, denominator), "tensor", 0)
    joint_max = jnp.maximum(maximum, other_max)
    own_scale = jnp.exp(maximum - joint_max)
    theirs = jnp.exp(other_max - joint_max)
    combined = kept_part * own_scale[..., None] + received_part * theirs[..., None]
    attended = combined / (denominator * own_scale + other_den * theirs)[..., None]
    attended = attended.astype(jnp.bfloat16)
    back = [attended[0]]
    for j in range(1, group_count):
        back.append(
            lax.ppermute(attended[j], "dp", [(i, (i + j) % group_count) for i in range(group_count)])
        )
    attended = jnp.stack(back)[(group_index - source) % group_count]
    tok_rows = residual_in.shape[0]
    head_out = attended.reshape(tensor_size, tok_rows, half_dim)
    owned = lax.all_to_all(head_out, "tensor", split_axis=0, concat_axis=0, tiled=True)
    owned = owned.transpose(1, 0, 2).reshape(tok_rows, tensor_size * half_dim)
    full_weight = lax.all_gather(out_weight, "tensor", axis=0, tiled=True)
    projected = jnp.dot(owned, full_weight, preferred_element_type=jnp.float32)
    hidden = residual_in.astype(jnp.float32) + projected
    normed = (
        hidden * lax.rsqrt(jnp.mean(hidden * hidden, axis=1, keepdims=True) + 1e-06) * norm_gain
    ).astype(jnp.bfloat16)
    capacity = max(2, tok_rows * TOP * 4 // (3 * EXPERTS))
    flat_routes = routes.reshape(-1)
    pair_count = flat_routes.shape[0]
    expert_ids = jnp.arange(EXPERTS, dtype=jnp.int32)
    one_hot = (flat_routes[:, None] == expert_ids[None, :]).astype(jnp.int32)
    earlier = jnp.cumsum(one_hot, axis=0) - one_hot
    rank_in_expert = jnp.sum(earlier * one_hot, axis=1)
    slot_of_pair = flat_routes * capacity + rank_in_expert
    slot_ids = jnp.arange(EXPERTS * capacity, dtype=jnp.int32)
    matches = slot_of_pair[None, :] == slot_ids[:, None]
    source_pair = jnp.sum(
        jnp.where(matches, jnp.arange(pair_count, dtype=jnp.int32)[None, :], 0), axis=1
    )
    filled = jnp.any(matches, axis=1)
    outgoing_rows = jnp.where(
        filled[:, None], normed[source_pair // TOP], jnp.zeros((), jnp.bfloat16)
    )
    experts_here = expert_gate.shape[0]
    width = normed.shape[1]
    outgoing_rows = outgoing_rows.reshape(tensor_size, experts_here, capacity, width)
    owner_slot = (flat_routes // experts_here) * capacity + rank_in_expert
    parity = flat_routes % experts_here
    routed = jnp.zeros((tok_rows, width), jnp.float32)
    slot_ids = jnp.arange(tensor_size * capacity, dtype=jnp.int32)
    flat_gates = route_gates.reshape(-1)
    for k in range(experts_here):
        fanned = jnp.broadcast_to(outgoing_rows[None, :, k], (group_count,) + outgoing_rows[:, k].shape)
        fanned = fanned.reshape((group_count * tensor_size, capacity, width))
        arrived_rows = lax.all_to_all(fanned, ("dp", "tensor"), split_axis=0, concat_axis=0, tiled=True)
        flat_rows = arrived_rows.reshape(-1, width)
        gate_part = jnp.dot(flat_rows, expert_gate[k], preferred_element_type=jnp.float32)
        up_part = jnp.dot(flat_rows, expert_up[k], preferred_element_type=jnp.float32)
        active = (jax.nn.silu(gate_part) * up_part).astype(jnp.bfloat16)
        partial_value = jnp.dot(active, expert_down[k], preferred_element_type=jnp.float32)
        partial_value = partial_value.astype(jnp.bfloat16).reshape(arrived_rows.shape)
        returned = lax.all_to_all(
            partial_value, ("dp", "tensor"), split_axis=0, concat_axis=0, tiled=True
        )
        hit = (owner_slot[:, None] == slot_ids[None, :]) & (parity == k)[:, None]
        coeff = jnp.where(hit, flat_gates[:, None], 0.0).reshape(tok_rows, TOP, -1).sum(axis=1)
        coeff = jnp.tile(coeff, (1, group_count))
        routed = routed + jnp.dot(
            coeff,
            returned.reshape(-1, width).astype(jnp.float32),
            precision=lax.Precision.HIGHEST,
            preferred_element_type=jnp.float32,
        )
    return hidden + routed


def solution(mesh):
    return jax.shard_map(
        shards,
        mesh=mesh,
        in_specs=(
            P("dp", "tensor", None),
            P("dp", None),
            P(),
            P(),
            P("dp", "tensor", None),
            P(("dp", "tensor"), None),
            P("tensor", None),
            P(),
            P(("dp", "tensor"), None),
            P(("dp", "tensor"), None),
            P("tensor", None, "dp"),
            P("tensor", None, "dp"),
            P("tensor", "dp", None),
        ),
        out_specs=P(("dp", "tensor"), None),
        check_vma=False,
    )
```

```python
import functools

import jax
import jax.numpy as jnp
from jax import lax
from jax.experimental import pallas as pl
from jax.experimental.pallas import tpu as pltpu
from jax.sharding import PartitionSpec as P

HEADS = 16
HD = 128
EXPERTS = 64
TOP = 6
PAGE = 64


def swapped(array, axis, stride):
    return lax.ppermute(array, axis, [(i, i ^ 1 << stride) for i in range(lax.axis_size(axis))])


def attn_body(scal_ref, q_ref, c_ref, f_ref, lo_ref, hi_ref, m_ref, d_ref, *, block_q, page_rows, head):
    item = pl.program_id(0)
    qb = pl.program_id(1)
    length = scal_ref[item]
    cache_offset = scal_ref[4]
    span_offset = scal_ref[5]
    scale = 1.0 / head**0.5
    q = q_ref[...]
    cached = c_ref[...]
    fresh = f_ref[...]
    dims = (((1,), (1,)), ((), ()))
    cs = lax.dot_general(q, cached[:, :head], dims, preferred_element_type=jnp.float32) * scale
    n = lax.broadcasted_iota(jnp.int32, cs.shape, 1)
    pos = (n // page_rows) * PAGE + cache_offset + n % page_rows
    cs = jnp.where(pos < length, cs, -1e30)
    ss = lax.dot_general(q, fresh[:, head:2 * head], dims, preferred_element_type=jnp.float32) * scale
    kpos = span_offset + lax.broadcasted_iota(jnp.int32, ss.shape, 1)
    qpos = qb * block_q + lax.broadcasted_iota(jnp.int32, ss.shape, 0)
    ss = jnp.where(kpos <= qpos, ss, -1e30)
    mx = jnp.maximum(jnp.max(cs, axis=1, keepdims=True), jnp.max(ss, axis=1, keepdims=True))
    cw = jnp.exp(cs - mx)
    sw = jnp.exp(ss - mx)
    den = jnp.sum(cw, axis=1, keepdims=True) + jnp.sum(sw, axis=1, keepdims=True)
    acc = jnp.dot(cw.astype(jnp.bfloat16), cached[:, head:], preferred_element_type=jnp.float32)
    acc = acc + jnp.dot(sw.astype(jnp.bfloat16), fresh[:, 2 * head:], preferred_element_type=jnp.float32)
    half = head // 2
    lo_ref[...] = acc[:, :half]
    hi_ref[...] = acc[:, half:]
    m_ref[...] = jnp.transpose(jnp.broadcast_to(mx, (block_q, 128)))[0:1, :]
    d_ref[...] = jnp.transpose(jnp.broadcast_to(den, (block_q, 128)))[0:1, :]


def attention_kernel(queries, cached, fresh, lengths, cache_offset, span_offset, interpret=False):
    items, span, head = queries.shape
    pages, page_rows = cached.shape[1], cached.shape[2]
    keys = pages * page_rows
    cached = cached.reshape(items, keys, cached.shape[3])
    fresh_rows = fresh.shape[1]
    block_q = 256
    scal = jnp.concatenate(
        [lengths.astype(jnp.int32), jnp.stack([cache_offset, span_offset]).astype(jnp.int32)]
    )
    body = functools.partial(attn_body, block_q=block_q, page_rows=page_rows, head=head)
    grid_spec = pltpu.PrefetchScalarGridSpec(
        num_scalar_prefetch=1,
        grid=(items, span // block_q),
        in_specs=[
            pl.BlockSpec((None, block_q, head), lambda i, b, s: (i, b, 0)),
            pl.BlockSpec((None, keys, 2 * head), lambda i, b, s: (i, 0, 0)),
            pl.BlockSpec((None, fresh_rows, 3 * head), lambda i, b, s: (i, 0, 0)),
        ],
        out_specs=[
            pl.BlockSpec((None, block_q, head // 2), lambda i, b, s: (i, b, 0)),
            pl.BlockSpec((None, block_q, head // 2), lambda i, b, s: (i, b, 0)),
            pl.BlockSpec((None, 1, block_q), lambda i, b, s: (i, 0, b)),
            pl.BlockSpec((None, 1, block_q), lambda i, b, s: (i, 0, b)),
        ],
    )
    lower, upper, mx, den = pl.pallas_call(
        body,
        grid_spec=grid_spec,
        out_shape=[
            jax.ShapeDtypeStruct((items, span, head // 2), jnp.float32),
            jax.ShapeDtypeStruct((items, span, head // 2), jnp.float32),
            jax.ShapeDtypeStruct((items, 1, span), jnp.float32),
            jax.ShapeDtypeStruct((items, 1, span), jnp.float32),
        ],
        interpret=interpret,
    )(scal, queries, cached, fresh)
    return lower, upper, mx[:, 0], den[:, 0]


def run_experts(slot_rows, expert_gate, expert_up, expert_down):
    gate_part = jnp.einsum(
        "secd,edf->secf", slot_rows, expert_gate, preferred_element_type=jnp.float32
    )
    up_part = jnp.einsum("secd,edf->secf", slot_rows, expert_up, preferred_element_type=jnp.float32)
    active = (jax.nn.silu(gate_part) * up_part).astype(jnp.bfloat16)
    return jnp.einsum("secf,efd->secd", active, expert_down, preferred_element_type=jnp.float32)


def shards(
    page_pool,
    page_table,
    destination,
    cache_len,
    new_tokens,
    residual_in,
    out_weight,
    norm_gain,
    routes,
    route_gates,
    expert_gate,
    expert_up,
    expert_down,
):
    tensor_size = lax.axis_size("tensor")
    group_count = lax.axis_size("dp")
    split_ways = max(1, tensor_size // HEADS)
    heads_here = max(1, HEADS // tensor_size)
    side_index = lax.axis_index("tensor") % split_ways
    group_index = lax.axis_index("dp")
    requests_here = page_table.shape[0]
    first_home = group_index * requests_here
    home_dest = lax.dynamic_slice_in_dim(destination, first_home, requests_here)
    dest_group = home_dest // requests_here
    request_ids = jnp.arange(requests_here, dtype=jnp.int32)
    shifts = jnp.arange(group_count, dtype=jnp.int32)
    work_req = jnp.sum(
        jnp.where(
            dest_group[None, :] == (group_index + shifts[:, None]) % group_count,
            request_ids[None, :],
            0,
        ),
        axis=1,
    )
    inverse = (
        jnp.zeros_like(destination)
        .at[destination]
        .set(jnp.arange(destination.shape[0], dtype=jnp.int32))
    )
    served = lax.dynamic_slice_in_dim(inverse, first_home, requests_here)
    source = served // requests_here
    send_slot = jnp.sum(
        jnp.where(
            source[None, :] == (group_index - shifts[:, None]) % group_count,
            request_ids[None, :],
            0,
        ),
        axis=1,
    )
    outgoing_tokens = new_tokens[send_slot]
    fresh = [outgoing_tokens[0]]
    for j in range(1, group_count):
        fresh.append(
            lax.ppermute(
                outgoing_tokens[j], "dp", [(i, (i - j) % group_count) for i in range(group_count)]
            )
        )
    new_tokens = jnp.stack(fresh)
    dense_cache = page_pool[page_table[work_req]]
    lengths = cache_len[first_home + work_req]
    fresh_per = new_tokens.shape[1] // heads_here
    span_len = fresh_per * split_ways
    rows_per_head = dense_cache.shape[2] // heads_here
    own_queries = new_tokens[:, :, :HD]
    other_queries = swapped(own_queries, "tensor", 0)
    lower_half = jnp.where(side_index == 0, own_queries, other_queries)
    upper_half = jnp.where(side_index == 0, other_queries, own_queries)
    queries = jnp.concatenate([lower_half, upper_half], axis=1)[:, None]

    head_results = attention_kernel(
        queries[:, 0],
        dense_cache,
        new_tokens,
        lengths,
        side_index * rows_per_head,
        side_index * fresh_per,
    )
    lower, upper, maximum, denominator = head_results
    half_dim = HD // 2
    given_part = jnp.where(side_index == 0, upper, lower)
    kept_part = jnp.where(side_index == 0, lower, upper)
    received_part, other_max, other_den = swapped((given_part, maximum, denominator), "tensor", 0)
    joint_max = jnp.maximum(maximum, other_max)
    own_scale = jnp.exp(maximum - joint_max)
    theirs = jnp.exp(other_max - joint_max)
    combined = kept_part * own_scale[..., None] + received_part * theirs[..., None]
    attended = combined / (denominator * own_scale + other_den * theirs)[..., None]
    attended = attended.astype(jnp.bfloat16)
    back = [attended[0]]
    for j in range(1, group_count):
        back.append(
            lax.ppermute(attended[j], "dp", [(i, (i + j) % group_count) for i in range(group_count)])
        )
    attended = jnp.stack(back)[(group_index - source) % group_count]
    tok_rows = residual_in.shape[0]
    head_out = attended.reshape(tensor_size, tok_rows, half_dim)
    owned = lax.all_to_all(head_out, "tensor", split_axis=0, concat_axis=0, tiled=True)
    owned = owned.transpose(1, 0, 2).reshape(tok_rows, tensor_size * half_dim)
    full_weight = lax.all_gather(out_weight, "tensor", axis=0, tiled=True)
    projected = jnp.dot(owned, full_weight, preferred_element_type=jnp.float32)
    hidden = residual_in.astype(jnp.float32) + projected
    normed = (
        hidden * lax.rsqrt(jnp.mean(hidden * hidden, axis=1, keepdims=True) + 1e-06) * norm_gain
    ).astype(jnp.bfloat16)
    capacity = max(2, tok_rows * TOP * 4 // (3 * EXPERTS))
    flat_routes = routes.reshape(-1)
    pair_count = flat_routes.shape[0]
    expert_ids = jnp.arange(EXPERTS, dtype=jnp.int32)
    one_hot = (flat_routes[:, None] == expert_ids[None, :]).astype(jnp.int32)
    earlier = jnp.cumsum(one_hot, axis=0) - one_hot
    rank_in_expert = jnp.sum(earlier * one_hot, axis=1)
    slot_of_pair = flat_routes * capacity + rank_in_expert
    slot_ids = jnp.arange(EXPERTS * capacity, dtype=jnp.int32)
    matches = slot_of_pair[None, :] == slot_ids[:, None]
    source_pair = jnp.sum(
        jnp.where(matches, jnp.arange(pair_count, dtype=jnp.int32)[None, :], 0), axis=1
    )
    filled = jnp.any(matches, axis=1)
    outgoing_rows = jnp.where(
        filled[:, None], normed[source_pair // TOP], jnp.zeros((), jnp.bfloat16)
    )
    experts_here = expert_gate.shape[0]
    width = normed.shape[1]
    outgoing_rows = outgoing_rows.reshape(tensor_size, experts_here, capacity, width)
    owner_slot = (flat_routes // experts_here) * capacity + rank_in_expert
    parity = flat_routes % experts_here
    routed = jnp.zeros((tok_rows, width), jnp.float32)
    slot_ids = jnp.arange(tensor_size * capacity, dtype=jnp.int32)
    flat_gates = route_gates.reshape(-1)
    for k in range(experts_here):
        fanned = jnp.broadcast_to(outgoing_rows[None, :, k], (group_count,) + outgoing_rows[:, k].shape)
        fanned = fanned.reshape((group_count * tensor_size, capacity, width))
        arrived_rows = lax.all_to_all(fanned, ("dp", "tensor"), split_axis=0, concat_axis=0, tiled=True)
        flat_rows = arrived_rows.reshape(-1, width)
        gate_part = jnp.dot(flat_rows, expert_gate[k], preferred_element_type=jnp.float32)
        up_part = jnp.dot(flat_rows, expert_up[k], preferred_element_type=jnp.float32)
        active = (jax.nn.silu(gate_part) * up_part).astype(jnp.bfloat16)
        partial_value = jnp.dot(active, expert_down[k], preferred_element_type=jnp.float32)
        partial_value = partial_value.astype(jnp.bfloat16).reshape(arrived_rows.shape)
        returned = lax.all_to_all(
            partial_value, ("dp", "tensor"), split_axis=0, concat_axis=0, tiled=True
        )
        hit = (owner_slot[:, None] == slot_ids[None, :]) & (parity == k)[:, None]
        coeff = jnp.where(hit, flat_gates[:, None], 0.0).reshape(tok_rows, TOP, -1).sum(axis=1)
        coeff = jnp.tile(coeff, (1, group_count))
        routed = routed + jnp.dot(
            coeff,
            returned.reshape(-1, width).astype(jnp.float32),
            precision=lax.Precision.HIGHEST,
            preferred_element_type=jnp.float32,
        )
    return hidden + routed


def solution(mesh):
    return jax.shard_map(
        shards,
        mesh=mesh,
        in_specs=(
            P("dp", "tensor", None),
            P("dp", None),
            P(),
            P(),
            P("dp", "tensor", None),
            P(("dp", "tensor"), None),
            P("tensor", None),
            P(),
            P(("dp", "tensor"), None),
            P(("dp", "tensor"), None),
            P("tensor", None, "dp"),
            P("tensor", None, "dp"),
            P("tensor", "dp", None),
        ),
        out_specs=P(("dp", "tensor"), None),
        check_vma=False,
    )
```

```python
import functools

import jax
import jax.numpy as jnp
from jax import lax
from jax.experimental import pallas as pl
from jax.experimental.pallas import tpu as pltpu
from jax.sharding import PartitionSpec as P

HEADS = 16
HD = 128
EXPERTS = 64
TOP = 6
PAGE = 64


def swapped(array, axis, stride):
    return lax.ppermute(array, axis, [(i, i ^ 1 << stride) for i in range(lax.axis_size(axis))])


def attn_body(scal_ref, q_ref, c_ref, f_ref, lo_ref, hi_ref, m_ref, d_ref, *, block_q, page_rows, head):
    item = pl.program_id(0)
    qb = pl.program_id(1)
    length = scal_ref[item]
    cache_offset = scal_ref[4]
    span_offset = scal_ref[5]
    scale = 1.0 / head**0.5
    q = q_ref[...]
    cached = c_ref[...]
    fresh = f_ref[...]
    dims = (((1,), (1,)), ((), ()))
    cs = lax.dot_general(q, cached[:, :head], dims, preferred_element_type=jnp.float32) * scale
    n = lax.broadcasted_iota(jnp.int32, cs.shape, 1)
    pos = (n // page_rows) * PAGE + cache_offset + n % page_rows
    cs = jnp.where(pos < length, cs, -1e30)
    ss = lax.dot_general(q, fresh[:, head:2 * head], dims, preferred_element_type=jnp.float32) * scale
    kpos = span_offset + lax.broadcasted_iota(jnp.int32, ss.shape, 1)
    qpos = qb * block_q + lax.broadcasted_iota(jnp.int32, ss.shape, 0)
    ss = jnp.where(kpos <= qpos, ss, -1e30)
    mx = jnp.maximum(jnp.max(cs, axis=1, keepdims=True), jnp.max(ss, axis=1, keepdims=True))
    cw = jnp.exp(cs - mx)
    sw = jnp.exp(ss - mx)
    den = jnp.sum(cw, axis=1, keepdims=True) + jnp.sum(sw, axis=1, keepdims=True)
    acc = jnp.dot(cw.astype(jnp.bfloat16), cached[:, head:], preferred_element_type=jnp.float32)
    acc = acc + jnp.dot(sw.astype(jnp.bfloat16), fresh[:, 2 * head:], preferred_element_type=jnp.float32)
    half = head // 2
    lo_ref[...] = acc[:, :half]
    hi_ref[...] = acc[:, half:]
    m_ref[...] = jnp.transpose(jnp.broadcast_to(mx, (block_q, 128)))[0:1, :]
    d_ref[...] = jnp.transpose(jnp.broadcast_to(den, (block_q, 128)))[0:1, :]


def attention_kernel(queries, cached, fresh, lengths, cache_offset, span_offset, interpret=False):
    items, span, head = queries.shape
    pages, page_rows = cached.shape[1], cached.shape[2]
    keys = pages * page_rows
    cached = cached.reshape(items, keys, cached.shape[3])
    fresh_rows = fresh.shape[1]
    block_q = 256
    scal = jnp.concatenate(
        [lengths.astype(jnp.int32), jnp.stack([cache_offset, span_offset]).astype(jnp.int32)]
    )
    body = functools.partial(attn_body, block_q=block_q, page_rows=page_rows, head=head)
    grid_spec = pltpu.PrefetchScalarGridSpec(
        num_scalar_prefetch=1,
        grid=(items, span // block_q),
        in_specs=[
            pl.BlockSpec((None, block_q, head), lambda i, b, s: (i, b, 0)),
            pl.BlockSpec((None, keys, 2 * head), lambda i, b, s: (i, 0, 0)),
            pl.BlockSpec((None, fresh_rows, 3 * head), lambda i, b, s: (i, 0, 0)),
        ],
        out_specs=[
            pl.BlockSpec((None, block_q, head // 2), lambda i, b, s: (i, b, 0)),
            pl.BlockSpec((None, block_q, head // 2), lambda i, b, s: (i, b, 0)),
            pl.BlockSpec((None, 1, block_q), lambda i, b, s: (i, 0, b)),
            pl.BlockSpec((None, 1, block_q), lambda i, b, s: (i, 0, b)),
        ],
    )
    lower, upper, mx, den = pl.pallas_call(
        body,
        grid_spec=grid_spec,
        out_shape=[
            jax.ShapeDtypeStruct((items, span, head // 2), jnp.float32),
            jax.ShapeDtypeStruct((items, span, head // 2), jnp.float32),
            jax.ShapeDtypeStruct((items, 1, span), jnp.float32),
            jax.ShapeDtypeStruct((items, 1, span), jnp.float32),
        ],
        interpret=interpret,
    )(scal, queries, cached, fresh)
    return lower, upper, mx[:, 0], den[:, 0]


def run_experts(slot_rows, expert_gate, expert_up, expert_down):
    gate_part = jnp.einsum(
        "secd,edf->secf", slot_rows, expert_gate, preferred_element_type=jnp.float32
    )
    up_part = jnp.einsum("secd,edf->secf", slot_rows, expert_up, preferred_element_type=jnp.float32)
    active = (jax.nn.silu(gate_part) * up_part).astype(jnp.bfloat16)
    return jnp.einsum("secf,efd->secd", active, expert_down, preferred_element_type=jnp.float32)


def shards(
    page_pool,
    page_table,
    destination,
    cache_len,
    new_tokens,
    residual_in,
    out_weight,
    norm_gain,
    routes,
    route_gates,
    expert_gate,
    expert_up,
    expert_down,
):
    tensor_size = lax.axis_size("tensor")
    group_count = lax.axis_size("dp")
    split_ways = max(1, tensor_size // HEADS)
    heads_here = max(1, HEADS // tensor_size)
    side_index = lax.axis_index("tensor") % split_ways
    group_index = lax.axis_index("dp")
    requests_here = page_table.shape[0]
    first_home = group_index * requests_here
    home_dest = lax.dynamic_slice_in_dim(destination, first_home, requests_here)
    dest_group = home_dest // requests_here
    request_ids = jnp.arange(requests_here, dtype=jnp.int32)
    shifts = jnp.arange(group_count, dtype=jnp.int32)
    work_req = jnp.sum(
        jnp.where(
            dest_group[None, :] == (group_index + shifts[:, None]) % group_count,
            request_ids[None, :],
            0,
        ),
        axis=1,
    )
    inverse = (
        jnp.zeros_like(destination)
        .at[destination]
        .set(jnp.arange(destination.shape[0], dtype=jnp.int32))
    )
    served = lax.dynamic_slice_in_dim(inverse, first_home, requests_here)
    source = served // requests_here
    send_slot = jnp.sum(
        jnp.where(
            source[None, :] == (group_index - shifts[:, None]) % group_count,
            request_ids[None, :],
            0,
        ),
        axis=1,
    )
    outgoing_tokens = new_tokens[send_slot]
    fresh = [outgoing_tokens[0]]
    for j in range(1, group_count):
        fresh.append(
            lax.ppermute(
                outgoing_tokens[j], "dp", [(i, (i - j) % group_count) for i in range(group_count)]
            )
        )
    new_tokens = jnp.stack(fresh)
    dense_cache = page_pool[page_table[work_req]]
    lengths = cache_len[first_home + work_req]
    fresh_per = new_tokens.shape[1] // heads_here
    span_len = fresh_per * split_ways
    rows_per_head = dense_cache.shape[2] // heads_here
    own_queries = new_tokens[:, :, :HD]
    other_queries = swapped(own_queries, "tensor", 0)
    lower_half = jnp.where(side_index == 0, own_queries, other_queries)
    upper_half = jnp.where(side_index == 0, other_queries, own_queries)
    queries = jnp.concatenate([lower_half, upper_half], axis=1)[:, None]

    head_results = attention_kernel(
        queries[:, 0],
        dense_cache,
        new_tokens,
        lengths,
        side_index * rows_per_head,
        side_index * fresh_per,
    )
    lower, upper, maximum, denominator = head_results
    half_dim = HD // 2
    given_part = jnp.where(side_index == 0, upper, lower)
    kept_part = jnp.where(side_index == 0, lower, upper)
    received_part, other_max, other_den = swapped((given_part, maximum, denominator), "tensor", 0)
    joint_max = jnp.maximum(maximum, other_max)
    own_scale = jnp.exp(maximum - joint_max)
    theirs = jnp.exp(other_max - joint_max)
    combined = kept_part * own_scale[..., None] + received_part * theirs[..., None]
    attended = combined / (denominator * own_scale + other_den * theirs)[..., None]
    attended = attended.astype(jnp.bfloat16)
    back = [attended[0]]
    for j in range(1, group_count):
        back.append(
            lax.ppermute(attended[j], "dp", [(i, (i + j) % group_count) for i in range(group_count)])
        )
    attended = jnp.stack(back)[(group_index - source) % group_count]
    tok_rows = residual_in.shape[0]
    head_out = attended.reshape(tensor_size, tok_rows, half_dim)
    owned = lax.all_to_all(head_out, "tensor", split_axis=0, concat_axis=0, tiled=True)
    owned = owned.transpose(1, 0, 2).reshape(tok_rows, tensor_size * half_dim)
    full_weight = lax.all_gather(out_weight, "tensor", axis=0, tiled=True)
    projected = jnp.dot(owned, full_weight, preferred_element_type=jnp.float32)
    hidden = residual_in.astype(jnp.float32) + projected
    normed = (
        hidden * lax.rsqrt(jnp.mean(hidden * hidden, axis=1, keepdims=True) + 1e-06) * norm_gain
    ).astype(jnp.bfloat16)
    capacity = max(2, tok_rows * TOP * 4 // (3 * EXPERTS))
    flat_routes = routes.reshape(-1)
    pair_count = flat_routes.shape[0]
    expert_ids = jnp.arange(EXPERTS, dtype=jnp.int32)
    one_hot = (flat_routes[:, None] == expert_ids[None, :]).astype(jnp.int32)
    earlier = jnp.cumsum(one_hot, axis=0) - one_hot
    rank_in_expert = jnp.sum(earlier * one_hot, axis=1)
    slot_of_pair = flat_routes * capacity + rank_in_expert
    slot_ids = jnp.arange(EXPERTS * capacity, dtype=jnp.int32)
    matches = slot_of_pair[None, :] == slot_ids[:, None]
    source_pair = jnp.sum(
        jnp.where(matches, jnp.arange(pair_count, dtype=jnp.int32)[None, :], 0), axis=1
    )
    filled = jnp.any(matches, axis=1)
    outgoing_rows = jnp.where(
        filled[:, None], normed[source_pair // TOP], jnp.zeros((), jnp.bfloat16)
    )
    experts_here = expert_gate.shape[0]
    width = normed.shape[1]
    outgoing_rows = outgoing_rows.reshape(tensor_size, experts_here, capacity, width)
    owner_slot = (flat_routes // experts_here) * capacity + rank_in_expert
    parity = flat_routes % experts_here
    routed = jnp.zeros((tok_rows, width), jnp.float32)
    slot_ids = jnp.arange(tensor_size * capacity, dtype=jnp.int32)
    flat_gates = route_gates.reshape(-1)
    for k in range(experts_here):
        fanned = jnp.broadcast_to(outgoing_rows[None, :, k], (group_count,) + outgoing_rows[:, k].shape)
        fanned = fanned.reshape((group_count * tensor_size, capacity, width))
        arrived_rows = lax.all_to_all(fanned, ("dp", "tensor"), split_axis=0, concat_axis=0, tiled=True)
        flat_rows = arrived_rows.reshape(-1, width)
        gate_part = jnp.dot(flat_rows, expert_gate[k], preferred_element_type=jnp.float32)
        up_part = jnp.dot(flat_rows, expert_up[k], preferred_element_type=jnp.float32)
        active = (jax.nn.silu(gate_part) * up_part).astype(jnp.bfloat16)
        partial_value = jnp.dot(active, expert_down[k], preferred_element_type=jnp.float32)
        partial_value = partial_value.astype(jnp.bfloat16).reshape(arrived_rows.shape)
        reduced = lax.psum_scatter(partial_value, "dp", scatter_dimension=0, tiled=True)
        returned = lax.all_to_all(reduced, "tensor", split_axis=0, concat_axis=0, tiled=True)
        hit = (owner_slot[:, None] == slot_ids[None, :]) & (parity == k)[:, None]
        coeff = jnp.where(hit, flat_gates[:, None], 0.0).reshape(tok_rows, TOP, -1).sum(axis=1)
        routed = routed + jnp.dot(
            coeff,
            returned.reshape(-1, width).astype(jnp.float32),
            precision=lax.Precision.HIGHEST,
            preferred_element_type=jnp.float32,
        )
    return hidden + routed


def solution(mesh):
    return jax.shard_map(
        shards,
        mesh=mesh,
        in_specs=(
            P("dp", "tensor", None),
            P("dp", None),
            P(),
            P(),
            P("dp", "tensor", None),
            P(("dp", "tensor"), None),
            P("tensor", None),
            P(),
            P(("dp", "tensor"), None),
            P(("dp", "tensor"), None),
            P("tensor", None, "dp"),
            P("tensor", None, "dp"),
            P("tensor", "dp", None),
        ),
        out_specs=P(("dp", "tensor"), None),
        check_vma=False,
    )
```

```python
import functools

import jax
import jax.numpy as jnp
from jax import lax
from jax.experimental import pallas as pl
from jax.experimental.pallas import tpu as pltpu
from jax.sharding import PartitionSpec as P

HEADS = 16
HD = 128
EXPERTS = 64
TOP = 6
PAGE = 64


def swapped(array, axis, stride):
    return lax.ppermute(array, axis, [(i, i ^ 1 << stride) for i in range(lax.axis_size(axis))])


def attn_body(scal_ref, q_ref, c_ref, f_ref, lo_ref, hi_ref, m_ref, d_ref, *, block_q, page_rows, head):
    item = pl.program_id(0)
    qb = pl.program_id(1)
    length = scal_ref[item]
    cache_offset = scal_ref[4]
    span_offset = scal_ref[5]
    scale = 1.0 / head**0.5
    q = q_ref[...]
    cached = c_ref[...]
    fresh = f_ref[...]
    dims = (((1,), (1,)), ((), ()))
    cs = lax.dot_general(q, cached[:, :head], dims, preferred_element_type=jnp.float32) * scale
    n = lax.broadcasted_iota(jnp.int32, cs.shape, 1)
    pos = (n // page_rows) * PAGE + cache_offset + n % page_rows
    cs = jnp.where(pos < length, cs, -1e30)
    ss = lax.dot_general(q, fresh[:, head:2 * head], dims, preferred_element_type=jnp.float32) * scale
    kpos = span_offset + lax.broadcasted_iota(jnp.int32, ss.shape, 1)
    qpos = qb * block_q + lax.broadcasted_iota(jnp.int32, ss.shape, 0)
    ss = jnp.where(kpos <= qpos, ss, -1e30)
    mx = jnp.maximum(jnp.max(cs, axis=1, keepdims=True), jnp.max(ss, axis=1, keepdims=True))
    cw = jnp.exp(cs - mx)
    sw = jnp.exp(ss - mx)
    den = jnp.sum(cw, axis=1, keepdims=True) + jnp.sum(sw, axis=1, keepdims=True)
    acc = jnp.dot(cw.astype(jnp.bfloat16), cached[:, head:], preferred_element_type=jnp.float32)
    acc = acc + jnp.dot(sw.astype(jnp.bfloat16), fresh[:, 2 * head:], preferred_element_type=jnp.float32)
    half = head // 2
    lo_ref[...] = acc[:, :half]
    hi_ref[...] = acc[:, half:]
    m_ref[...] = jnp.transpose(jnp.broadcast_to(mx, (block_q, 128)))[0:1, :]
    d_ref[...] = jnp.transpose(jnp.broadcast_to(den, (block_q, 128)))[0:1, :]


def attention_kernel(queries, cached, fresh, lengths, cache_offset, span_offset, interpret=False):
    items, span, head = queries.shape
    pages, page_rows = cached.shape[1], cached.shape[2]
    keys = pages * page_rows
    cached = cached.reshape(items, keys, cached.shape[3])
    fresh_rows = fresh.shape[1]
    block_q = 256
    scal = jnp.concatenate(
        [lengths.astype(jnp.int32), jnp.stack([cache_offset, span_offset]).astype(jnp.int32)]
    )
    body = functools.partial(attn_body, block_q=block_q, page_rows=page_rows, head=head)
    grid_spec = pltpu.PrefetchScalarGridSpec(
        num_scalar_prefetch=1,
        grid=(items, span // block_q),
        in_specs=[
            pl.BlockSpec((None, block_q, head), lambda i, b, s: (i, b, 0)),
            pl.BlockSpec((None, keys, 2 * head), lambda i, b, s: (i, 0, 0)),
            pl.BlockSpec((None, fresh_rows, 3 * head), lambda i, b, s: (i, 0, 0)),
        ],
        out_specs=[
            pl.BlockSpec((None, block_q, head // 2), lambda i, b, s: (i, b, 0)),
            pl.BlockSpec((None, block_q, head // 2), lambda i, b, s: (i, b, 0)),
            pl.BlockSpec((None, 1, block_q), lambda i, b, s: (i, 0, b)),
            pl.BlockSpec((None, 1, block_q), lambda i, b, s: (i, 0, b)),
        ],
    )
    lower, upper, mx, den = pl.pallas_call(
        body,
        grid_spec=grid_spec,
        out_shape=[
            jax.ShapeDtypeStruct((items, span, head // 2), jnp.float32),
            jax.ShapeDtypeStruct((items, span, head // 2), jnp.float32),
            jax.ShapeDtypeStruct((items, 1, span), jnp.float32),
            jax.ShapeDtypeStruct((items, 1, span), jnp.float32),
        ],
        interpret=interpret,
    )(scal, queries, cached, fresh)
    return lower, upper, mx[:, 0], den[:, 0]


def run_experts(slot_rows, expert_gate, expert_up, expert_down):
    gate_part = jnp.einsum(
        "secd,edf->secf", slot_rows, expert_gate, preferred_element_type=jnp.float32
    )
    up_part = jnp.einsum("secd,edf->secf", slot_rows, expert_up, preferred_element_type=jnp.float32)
    active = (jax.nn.silu(gate_part) * up_part).astype(jnp.bfloat16)
    return jnp.einsum("secf,efd->secd", active, expert_down, preferred_element_type=jnp.float32)


def shards(
    page_pool,
    page_table,
    destination,
    cache_len,
    new_tokens,
    residual_in,
    out_weight,
    norm_gain,
    routes,
    route_gates,
    expert_gate,
    expert_up,
    expert_down,
):
    tensor_size = lax.axis_size("tensor")
    group_count = lax.axis_size("dp")
    split_ways = max(1, tensor_size // HEADS)
    heads_here = max(1, HEADS // tensor_size)
    side_index = lax.axis_index("tensor") % split_ways
    group_index = lax.axis_index("dp")
    requests_here = page_table.shape[0]
    first_home = group_index * requests_here
    home_dest = lax.dynamic_slice_in_dim(destination, first_home, requests_here)
    dest_group = home_dest // requests_here
    request_ids = jnp.arange(requests_here, dtype=jnp.int32)
    shifts = jnp.arange(group_count, dtype=jnp.int32)
    work_req = jnp.sum(
        jnp.where(
            dest_group[None, :] == (group_index + shifts[:, None]) % group_count,
            request_ids[None, :],
            0,
        ),
        axis=1,
    )
    inverse = (
        jnp.zeros_like(destination)
        .at[destination]
        .set(jnp.arange(destination.shape[0], dtype=jnp.int32))
    )
    served = lax.dynamic_slice_in_dim(inverse, first_home, requests_here)
    source = served // requests_here
    send_slot = jnp.sum(
        jnp.where(
            source[None, :] == (group_index - shifts[:, None]) % group_count,
            request_ids[None, :],
            0,
        ),
        axis=1,
    )
    outgoing_tokens = new_tokens[send_slot]
    fresh = [outgoing_tokens[0]]
    for j in range(1, group_count):
        fresh.append(
            lax.ppermute(
                outgoing_tokens[j], "dp", [(i, (i - j) % group_count) for i in range(group_count)]
            )
        )
    new_tokens = jnp.stack(fresh)
    dense_cache = page_pool[page_table[work_req]]
    lengths = cache_len[first_home + work_req]
    fresh_per = new_tokens.shape[1] // heads_here
    span_len = fresh_per * split_ways
    rows_per_head = dense_cache.shape[2] // heads_here
    own_queries = new_tokens[:, :, :HD]
    other_queries = swapped(own_queries, "tensor", 0)
    lower_half = jnp.where(side_index == 0, own_queries, other_queries)
    upper_half = jnp.where(side_index == 0, other_queries, own_queries)
    queries = jnp.concatenate([lower_half, upper_half], axis=1)[:, None]

    head_results = attention_kernel(
        queries[:, 0],
        dense_cache,
        new_tokens,
        lengths,
        side_index * rows_per_head,
        side_index * fresh_per,
    )
    lower, upper, maximum, denominator = head_results
    half_dim = HD // 2
    given_part = jnp.where(side_index == 0, upper, lower)
    kept_part = jnp.where(side_index == 0, lower, upper)
    received_part, other_max, other_den = swapped((given_part, maximum, denominator), "tensor", 0)
    joint_max = jnp.maximum(maximum, other_max)
    own_scale = jnp.exp(maximum - joint_max)
    theirs = jnp.exp(other_max - joint_max)
    combined = kept_part * own_scale[..., None] + received_part * theirs[..., None]
    attended = combined / (denominator * own_scale + other_den * theirs)[..., None]
    attended = attended.astype(jnp.bfloat16)
    back = [attended[0]]
    for j in range(1, group_count):
        back.append(
            lax.ppermute(attended[j], "dp", [(i, (i + j) % group_count) for i in range(group_count)])
        )
    attended = jnp.stack(back)[(group_index - source) % group_count]
    tok_rows = residual_in.shape[0]
    head_out = attended.reshape(tensor_size, tok_rows, half_dim)
    owned = lax.all_to_all(head_out, "tensor", split_axis=0, concat_axis=0, tiled=True)
    owned = owned.transpose(1, 0, 2).reshape(tok_rows, tensor_size * half_dim)
    full_weight = lax.all_gather(out_weight, "tensor", axis=0, tiled=True)
    projected = jnp.dot(owned, full_weight, preferred_element_type=jnp.float32)
    hidden = residual_in.astype(jnp.float32) + projected
    normed = (
        hidden * lax.rsqrt(jnp.mean(hidden * hidden, axis=1, keepdims=True) + 1e-06) * norm_gain
    ).astype(jnp.bfloat16)
    capacity = max(2, tok_rows * TOP * 4 // (3 * EXPERTS))
    flat_routes = routes.reshape(-1)
    pair_count = flat_routes.shape[0]
    expert_ids = jnp.arange(EXPERTS, dtype=jnp.int32)
    one_hot = (flat_routes[:, None] == expert_ids[None, :]).astype(jnp.int32)
    earlier = jnp.cumsum(one_hot, axis=0) - one_hot
    rank_in_expert = jnp.sum(earlier * one_hot, axis=1)
    slot_of_pair = flat_routes * capacity + rank_in_expert
    slot_ids = jnp.arange(EXPERTS * capacity, dtype=jnp.int32)
    matches = slot_of_pair[None, :] == slot_ids[:, None]
    source_pair = jnp.sum(
        jnp.where(matches, jnp.arange(pair_count, dtype=jnp.int32)[None, :], 0), axis=1
    )
    filled = jnp.any(matches, axis=1)
    outgoing_rows = jnp.where(
        filled[:, None], normed[source_pair // TOP], jnp.zeros((), jnp.bfloat16)
    )
    experts_here = expert_gate.shape[0]
    width = normed.shape[1]
    outgoing_rows = outgoing_rows.reshape(tensor_size, experts_here, capacity, width)
    owner_slot = (flat_routes // experts_here) * capacity + rank_in_expert
    parity = flat_routes % experts_here
    routed = jnp.zeros((tok_rows, width), jnp.float32)
    slot_ids = jnp.arange(tensor_size * capacity, dtype=jnp.int32)
    flat_gates = route_gates.reshape(-1)
    for k in range(experts_here):
        same_group = lax.all_to_all(
            outgoing_rows[:, k], "tensor", split_axis=0, concat_axis=0, tiled=True
        )
        arrived_rows = lax.all_gather(same_group, "dp", axis=0, tiled=True)
        flat_rows = arrived_rows.reshape(-1, width)
        gate_part = jnp.dot(flat_rows, expert_gate[k], preferred_element_type=jnp.float32)
        up_part = jnp.dot(flat_rows, expert_up[k], preferred_element_type=jnp.float32)
        active = (jax.nn.silu(gate_part) * up_part).astype(jnp.bfloat16)
        partial_value = jnp.dot(active, expert_down[k], preferred_element_type=jnp.float32)
        partial_value = partial_value.astype(jnp.bfloat16).reshape(arrived_rows.shape)
        reduced = lax.psum_scatter(partial_value, "dp", scatter_dimension=0, tiled=True)
        returned = lax.all_to_all(reduced, "tensor", split_axis=0, concat_axis=0, tiled=True)
        hit = (owner_slot[:, None] == slot_ids[None, :]) & (parity == k)[:, None]
        coeff = jnp.where(hit, flat_gates[:, None], 0.0).reshape(tok_rows, TOP, -1).sum(axis=1)
        routed = routed + jnp.dot(
            coeff,
            returned.reshape(-1, width).astype(jnp.float32),
            precision=lax.Precision.HIGHEST,
            preferred_element_type=jnp.float32,
        )
    return hidden + routed


def solution(mesh):
    return jax.shard_map(
        shards,
        mesh=mesh,
        in_specs=(
            P("dp", "tensor", None),
            P("dp", None),
            P(),
            P(),
            P("dp", "tensor", None),
            P(("dp", "tensor"), None),
            P("tensor", None),
            P(),
            P(("dp", "tensor"), None),
            P(("dp", "tensor"), None),
            P("tensor", None, "dp"),
            P("tensor", None, "dp"),
            P("tensor", "dp", None),
        ),
        out_specs=P(("dp", "tensor"), None),
        check_vma=False,
    )
```

```python
import functools

import jax
import jax.numpy as jnp
from jax import lax
from jax.experimental import pallas as pl
from jax.experimental.pallas import tpu as pltpu
from jax.sharding import PartitionSpec as P

HEADS = 16
HD = 128
EXPERTS = 64
TOP = 6
PAGE = 64


def swapped(array, axis, stride):
    return lax.ppermute(array, axis, [(i, i ^ 1 << stride) for i in range(lax.axis_size(axis))])


def attn_body(scal_ref, q_ref, c_ref, f_ref, lo_ref, hi_ref, m_ref, d_ref, *, block_q, page_rows, head):
    item = pl.program_id(0)
    qb = pl.program_id(1)
    length = scal_ref[item]
    cache_offset = scal_ref[4]
    span_offset = scal_ref[5]
    scale = 1.0 / head**0.5
    q = q_ref[...]
    cached = c_ref[...]
    fresh = f_ref[...]
    dims = (((1,), (1,)), ((), ()))
    cs = lax.dot_general(q, cached[:, :head], dims, preferred_element_type=jnp.float32) * scale
    n = lax.broadcasted_iota(jnp.int32, cs.shape, 1)
    pos = (n // page_rows) * PAGE + cache_offset + n % page_rows
    cs = jnp.where(pos < length, cs, -1e30)
    ss = lax.dot_general(q, fresh[:, head:2 * head], dims, preferred_element_type=jnp.float32) * scale
    kpos = span_offset + lax.broadcasted_iota(jnp.int32, ss.shape, 1)
    qpos = qb * block_q + lax.broadcasted_iota(jnp.int32, ss.shape, 0)
    ss = jnp.where(kpos <= qpos, ss, -1e30)
    mx = jnp.maximum(jnp.max(cs, axis=1, keepdims=True), jnp.max(ss, axis=1, keepdims=True))
    cw = jnp.exp(cs - mx)
    sw = jnp.exp(ss - mx)
    den = jnp.sum(cw, axis=1, keepdims=True) + jnp.sum(sw, axis=1, keepdims=True)
    acc = jnp.dot(cw.astype(jnp.bfloat16), cached[:, head:], preferred_element_type=jnp.float32)
    acc = acc + jnp.dot(sw.astype(jnp.bfloat16), fresh[:, 2 * head:], preferred_element_type=jnp.float32)
    half = head // 2
    lo_ref[...] = acc[:, :half]
    hi_ref[...] = acc[:, half:]
    m_ref[...] = jnp.transpose(jnp.broadcast_to(mx, (block_q, 128)))[0:1, :]
    d_ref[...] = jnp.transpose(jnp.broadcast_to(den, (block_q, 128)))[0:1, :]


def attention_kernel(queries, cached, fresh, lengths, cache_offset, span_offset, interpret=False):
    items, span, head = queries.shape
    pages, page_rows = cached.shape[1], cached.shape[2]
    keys = pages * page_rows
    cached = cached.reshape(items, keys, cached.shape[3])
    fresh_rows = fresh.shape[1]
    block_q = 256
    scal = jnp.concatenate(
        [lengths.astype(jnp.int32), jnp.stack([cache_offset, span_offset]).astype(jnp.int32)]
    )
    body = functools.partial(attn_body, block_q=block_q, page_rows=page_rows, head=head)
    grid_spec = pltpu.PrefetchScalarGridSpec(
        num_scalar_prefetch=1,
        grid=(items, span // block_q),
        in_specs=[
            pl.BlockSpec((None, block_q, head), lambda i, b, s: (i, b, 0)),
            pl.BlockSpec((None, keys, 2 * head), lambda i, b, s: (i, 0, 0)),
            pl.BlockSpec((None, fresh_rows, 3 * head), lambda i, b, s: (i, 0, 0)),
        ],
        out_specs=[
            pl.BlockSpec((None, block_q, head // 2), lambda i, b, s: (i, b, 0)),
            pl.BlockSpec((None, block_q, head // 2), lambda i, b, s: (i, b, 0)),
            pl.BlockSpec((None, 1, block_q), lambda i, b, s: (i, 0, b)),
            pl.BlockSpec((None, 1, block_q), lambda i, b, s: (i, 0, b)),
        ],
    )
    lower, upper, mx, den = pl.pallas_call(
        body,
        grid_spec=grid_spec,
        out_shape=[
            jax.ShapeDtypeStruct((items, span, head // 2), jnp.float32),
            jax.ShapeDtypeStruct((items, span, head // 2), jnp.float32),
            jax.ShapeDtypeStruct((items, 1, span), jnp.float32),
            jax.ShapeDtypeStruct((items, 1, span), jnp.float32),
        ],
        interpret=interpret,
    )(scal, queries, cached, fresh)
    return lower, upper, mx[:, 0], den[:, 0]


def run_experts(slot_rows, expert_gate, expert_up, expert_down):
    gate_part = jnp.einsum(
        "secd,edf->secf", slot_rows, expert_gate, preferred_element_type=jnp.float32
    )
    up_part = jnp.einsum("secd,edf->secf", slot_rows, expert_up, preferred_element_type=jnp.float32)
    active = (jax.nn.silu(gate_part) * up_part).astype(jnp.bfloat16)
    return jnp.einsum("secf,efd->secd", active, expert_down, preferred_element_type=jnp.float32)


def shards(
    page_pool,
    page_table,
    destination,
    cache_len,
    new_tokens,
    residual_in,
    out_weight,
    norm_gain,
    routes,
    route_gates,
    expert_gate,
    expert_up,
    expert_down,
):
    tensor_size = lax.axis_size("tensor")
    group_count = lax.axis_size("dp")
    split_ways = max(1, tensor_size // HEADS)
    heads_here = max(1, HEADS // tensor_size)
    side_index = lax.axis_index("tensor") % split_ways
    group_index = lax.axis_index("dp")
    requests_here = page_table.shape[0]
    first_home = group_index * requests_here
    home_dest = lax.dynamic_slice_in_dim(destination, first_home, requests_here)
    dest_group = home_dest // requests_here
    request_ids = jnp.arange(requests_here, dtype=jnp.int32)
    shifts = jnp.arange(group_count, dtype=jnp.int32)
    work_req = jnp.sum(
        jnp.where(
            dest_group[None, :] == (group_index + shifts[:, None]) % group_count,
            request_ids[None, :],
            0,
        ),
        axis=1,
    )
    inverse = (
        jnp.zeros_like(destination)
        .at[destination]
        .set(jnp.arange(destination.shape[0], dtype=jnp.int32))
    )
    served = lax.dynamic_slice_in_dim(inverse, first_home, requests_here)
    source = served // requests_here
    send_slot = jnp.sum(
        jnp.where(
            source[None, :] == (group_index - shifts[:, None]) % group_count,
            request_ids[None, :],
            0,
        ),
        axis=1,
    )
    outgoing_tokens = new_tokens[send_slot]
    fresh = [outgoing_tokens[0]]
    for j in range(1, group_count):
        fresh.append(
            lax.ppermute(
                outgoing_tokens[j], "dp", [(i, (i - j) % group_count) for i in range(group_count)]
            )
        )
    new_tokens = jnp.stack(fresh)
    dense_cache = page_pool[page_table[work_req]]
    lengths = cache_len[first_home + work_req]
    fresh_per = new_tokens.shape[1] // heads_here
    span_len = fresh_per * split_ways
    rows_per_head = dense_cache.shape[2] // heads_here
    own_queries = new_tokens[:, :, :HD]
    other_queries = swapped(own_queries, "tensor", 0)
    lower_half = jnp.where(side_index == 0, own_queries, other_queries)
    upper_half = jnp.where(side_index == 0, other_queries, own_queries)
    queries = jnp.concatenate([lower_half, upper_half], axis=1)[:, None]

    head_results = attention_kernel(
        queries[:, 0],
        dense_cache,
        new_tokens,
        lengths,
        side_index * rows_per_head,
        side_index * fresh_per,
    )
    lower, upper, maximum, denominator = head_results
    half_dim = HD // 2
    given_part = jnp.where(side_index == 0, upper, lower)
    kept_part = jnp.where(side_index == 0, lower, upper)
    received_part, other_max, other_den = swapped((given_part, maximum, denominator), "tensor", 0)
    joint_max = jnp.maximum(maximum, other_max)
    own_scale = jnp.exp(maximum - joint_max)
    theirs = jnp.exp(other_max - joint_max)
    combined = kept_part * own_scale[..., None] + received_part * theirs[..., None]
    attended = combined / (denominator * own_scale + other_den * theirs)[..., None]
    attended = attended.astype(jnp.bfloat16)
    back = [attended[0]]
    for j in range(1, group_count):
        back.append(
            lax.ppermute(attended[j], "dp", [(i, (i + j) % group_count) for i in range(group_count)])
        )
    attended = jnp.stack(back)[(group_index - source) % group_count]
    tok_rows = residual_in.shape[0]
    head_out = attended.reshape(tensor_size, tok_rows, half_dim)
    owned = lax.all_to_all(head_out, "tensor", split_axis=0, concat_axis=0, tiled=True)
    owned = owned.transpose(1, 0, 2).reshape(tok_rows, tensor_size * half_dim)
    full_weight = lax.all_gather(out_weight, "tensor", axis=0, tiled=True)
    projected = jnp.dot(owned, full_weight, preferred_element_type=jnp.float32)
    hidden = residual_in.astype(jnp.float32) + projected
    normed = (
        hidden * lax.rsqrt(jnp.mean(hidden * hidden, axis=1, keepdims=True) + 1e-06) * norm_gain
    ).astype(jnp.bfloat16)
    capacity = max(2, tok_rows * TOP * 4 // (3 * EXPERTS))
    flat_routes = routes.reshape(-1)
    pair_count = flat_routes.shape[0]
    expert_ids = jnp.arange(EXPERTS, dtype=jnp.int32)
    one_hot = (flat_routes[:, None] == expert_ids[None, :]).astype(jnp.int32)
    earlier = jnp.cumsum(one_hot, axis=0) - one_hot
    rank_in_expert = jnp.sum(earlier * one_hot, axis=1)
    slot_of_pair = flat_routes * capacity + rank_in_expert
    slot_ids = jnp.arange(EXPERTS * capacity, dtype=jnp.int32)
    matches = slot_of_pair[None, :] == slot_ids[:, None]
    source_pair = jnp.sum(
        jnp.where(matches, jnp.arange(pair_count, dtype=jnp.int32)[None, :], 0), axis=1
    )
    filled = jnp.any(matches, axis=1)
    outgoing_rows = jnp.where(
        filled[:, None], normed[source_pair // TOP], jnp.zeros((), jnp.bfloat16)
    )
    experts_here = expert_gate.shape[0]
    width = normed.shape[1]
    outgoing_rows = outgoing_rows.reshape(tensor_size, experts_here, capacity, width)
    owner_slot = (flat_routes // experts_here) * capacity + rank_in_expert
    parity = flat_routes % experts_here
    routed = jnp.zeros((tok_rows, width), jnp.float32)
    slot_ids = jnp.arange(tensor_size * capacity, dtype=jnp.int32)
    flat_gates = route_gates.reshape(-1)
    for k in range(experts_here):
        if k == 0:
            fanned = jnp.broadcast_to(outgoing_rows[None, :, k], (group_count,) + outgoing_rows[:, k].shape)
            fanned = fanned.reshape((group_count * tensor_size, capacity, width))
            arrived_rows = lax.all_to_all(
                fanned, ("dp", "tensor"), split_axis=0, concat_axis=0, tiled=True
            )
        else:
            same_group = lax.all_to_all(
                outgoing_rows[:, k], "tensor", split_axis=0, concat_axis=0, tiled=True
            )
            arrived_rows = lax.all_gather(same_group, "dp", axis=0, tiled=True)
        flat_rows = arrived_rows.reshape(-1, width)
        gate_part = jnp.dot(flat_rows, expert_gate[k], preferred_element_type=jnp.float32)
        up_part = jnp.dot(flat_rows, expert_up[k], preferred_element_type=jnp.float32)
        active = (jax.nn.silu(gate_part) * up_part).astype(jnp.bfloat16)
        partial_value = jnp.dot(active, expert_down[k], preferred_element_type=jnp.float32)
        partial_value = partial_value.astype(jnp.bfloat16).reshape(arrived_rows.shape)
        reduced = lax.psum_scatter(partial_value, "dp", scatter_dimension=0, tiled=True)
        returned = lax.all_to_all(reduced, "tensor", split_axis=0, concat_axis=0, tiled=True)
        hit = (owner_slot[:, None] == slot_ids[None, :]) & (parity == k)[:, None]
        coeff = jnp.where(hit, flat_gates[:, None], 0.0).reshape(tok_rows, TOP, -1).sum(axis=1)
        routed = routed + jnp.dot(
            coeff,
            returned.reshape(-1, width).astype(jnp.float32),
            precision=lax.Precision.HIGHEST,
            preferred_element_type=jnp.float32,
        )
    return hidden + routed


def solution(mesh):
    return jax.shard_map(
        shards,
        mesh=mesh,
        in_specs=(
            P("dp", "tensor", None),
            P("dp", None),
            P(),
            P(),
            P("dp", "tensor", None),
            P(("dp", "tensor"), None),
            P("tensor", None),
            P(),
            P(("dp", "tensor"), None),
            P(("dp", "tensor"), None),
            P("tensor", None, "dp"),
            P("tensor", None, "dp"),
            P("tensor", "dp", None),
        ),
        out_specs=P(("dp", "tensor"), None),
        check_vma=False,
    )
```

```python
import functools

import jax
import jax.numpy as jnp
from jax import lax
from jax.experimental import pallas as pl
from jax.experimental.pallas import tpu as pltpu
from jax.sharding import PartitionSpec as P

HEADS = 16
HD = 128
EXPERTS = 64
TOP = 6
PAGE = 64


def swapped(array, axis, stride):
    return lax.ppermute(array, axis, [(i, i ^ 1 << stride) for i in range(lax.axis_size(axis))])


def attn_body(scal_ref, q_ref, c_ref, f_ref, lo_ref, hi_ref, m_ref, d_ref, *, block_q, page_rows, head):
    item = pl.program_id(0)
    qb = pl.program_id(1)
    length = scal_ref[item]
    cache_offset = scal_ref[4]
    span_offset = scal_ref[5]
    scale = 1.0 / head**0.5
    q = q_ref[...]
    cached = c_ref[...]
    fresh = f_ref[...]
    dims = (((1,), (1,)), ((), ()))
    cs = lax.dot_general(q, cached[:, :head], dims, preferred_element_type=jnp.float32) * scale
    n = lax.broadcasted_iota(jnp.int32, cs.shape, 1)
    pos = (n // page_rows) * PAGE + cache_offset + n % page_rows
    cs = jnp.where(pos < length, cs, -1e30)
    ss = lax.dot_general(q, fresh[:, head:2 * head], dims, preferred_element_type=jnp.float32) * scale
    kpos = span_offset + lax.broadcasted_iota(jnp.int32, ss.shape, 1)
    qpos = qb * block_q + lax.broadcasted_iota(jnp.int32, ss.shape, 0)
    ss = jnp.where(kpos <= qpos, ss, -1e30)
    mx = jnp.maximum(jnp.max(cs, axis=1, keepdims=True), jnp.max(ss, axis=1, keepdims=True))
    cw = jnp.exp(cs - mx)
    sw = jnp.exp(ss - mx)
    den = jnp.sum(cw, axis=1, keepdims=True) + jnp.sum(sw, axis=1, keepdims=True)
    acc = jnp.dot(cw.astype(jnp.bfloat16), cached[:, head:], preferred_element_type=jnp.float32)
    acc = acc + jnp.dot(sw.astype(jnp.bfloat16), fresh[:, 2 * head:], preferred_element_type=jnp.float32)
    half = head // 2
    lo_ref[...] = acc[:, :half]
    hi_ref[...] = acc[:, half:]
    m_ref[...] = jnp.transpose(jnp.broadcast_to(mx, (block_q, 128)))[0:1, :]
    d_ref[...] = jnp.transpose(jnp.broadcast_to(den, (block_q, 128)))[0:1, :]


def attention_kernel(queries, cached, fresh, lengths, cache_offset, span_offset, interpret=False):
    items, span, head = queries.shape
    pages, page_rows = cached.shape[1], cached.shape[2]
    keys = pages * page_rows
    cached = cached.reshape(items, keys, cached.shape[3])
    fresh_rows = fresh.shape[1]
    block_q = 256
    scal = jnp.concatenate(
        [lengths.astype(jnp.int32), jnp.stack([cache_offset, span_offset]).astype(jnp.int32)]
    )
    body = functools.partial(attn_body, block_q=block_q, page_rows=page_rows, head=head)
    grid_spec = pltpu.PrefetchScalarGridSpec(
        num_scalar_prefetch=1,
        grid=(items, span // block_q),
        in_specs=[
            pl.BlockSpec((None, block_q, head), lambda i, b, s: (i, b, 0)),
            pl.BlockSpec((None, keys, 2 * head), lambda i, b, s: (i, 0, 0)),
            pl.BlockSpec((None, fresh_rows, 3 * head), lambda i, b, s: (i, 0, 0)),
        ],
        out_specs=[
            pl.BlockSpec((None, block_q, head // 2), lambda i, b, s: (i, b, 0)),
            pl.BlockSpec((None, block_q, head // 2), lambda i, b, s: (i, b, 0)),
            pl.BlockSpec((None, 1, block_q), lambda i, b, s: (i, 0, b)),
            pl.BlockSpec((None, 1, block_q), lambda i, b, s: (i, 0, b)),
        ],
    )
    lower, upper, mx, den = pl.pallas_call(
        body,
        grid_spec=grid_spec,
        out_shape=[
            jax.ShapeDtypeStruct((items, span, head // 2), jnp.float32),
            jax.ShapeDtypeStruct((items, span, head // 2), jnp.float32),
            jax.ShapeDtypeStruct((items, 1, span), jnp.float32),
            jax.ShapeDtypeStruct((items, 1, span), jnp.float32),
        ],
        interpret=interpret,
    )(scal, queries, cached, fresh)
    return lower, upper, mx[:, 0], den[:, 0]


def run_experts(slot_rows, expert_gate, expert_up, expert_down):
    gate_part = jnp.einsum(
        "secd,edf->secf", slot_rows, expert_gate, preferred_element_type=jnp.float32
    )
    up_part = jnp.einsum("secd,edf->secf", slot_rows, expert_up, preferred_element_type=jnp.float32)
    active = (jax.nn.silu(gate_part) * up_part).astype(jnp.bfloat16)
    return jnp.einsum("secf,efd->secd", active, expert_down, preferred_element_type=jnp.float32)


def shards(
    page_pool,
    page_table,
    destination,
    cache_len,
    new_tokens,
    residual_in,
    out_weight,
    norm_gain,
    routes,
    route_gates,
    expert_gate,
    expert_up,
    expert_down,
):
    tensor_size = lax.axis_size("tensor")
    group_count = lax.axis_size("dp")
    split_ways = max(1, tensor_size // HEADS)
    heads_here = max(1, HEADS // tensor_size)
    side_index = lax.axis_index("tensor") % split_ways
    group_index = lax.axis_index("dp")
    requests_here = page_table.shape[0]
    first_home = group_index * requests_here
    home_dest = lax.dynamic_slice_in_dim(destination, first_home, requests_here)
    dest_group = home_dest // requests_here
    request_ids = jnp.arange(requests_here, dtype=jnp.int32)
    shifts = jnp.arange(group_count, dtype=jnp.int32)
    work_req = jnp.sum(
        jnp.where(
            dest_group[None, :] == (group_index + shifts[:, None]) % group_count,
            request_ids[None, :],
            0,
        ),
        axis=1,
    )
    inverse = (
        jnp.zeros_like(destination)
        .at[destination]
        .set(jnp.arange(destination.shape[0], dtype=jnp.int32))
    )
    served = lax.dynamic_slice_in_dim(inverse, first_home, requests_here)
    source = served // requests_here
    send_slot = jnp.sum(
        jnp.where(
            source[None, :] == (group_index - shifts[:, None]) % group_count,
            request_ids[None, :],
            0,
        ),
        axis=1,
    )
    outgoing_tokens = new_tokens[send_slot]
    fresh = [outgoing_tokens[0]]
    for j in range(1, group_count):
        fresh.append(
            lax.ppermute(
                outgoing_tokens[j], "dp", [(i, (i - j) % group_count) for i in range(group_count)]
            )
        )
    new_tokens = jnp.stack(fresh)
    dense_cache = page_pool[page_table[work_req]]
    lengths = cache_len[first_home + work_req]
    fresh_per = new_tokens.shape[1] // heads_here
    span_len = fresh_per * split_ways
    rows_per_head = dense_cache.shape[2] // heads_here
    own_queries = new_tokens[:, :, :HD]
    other_queries = swapped(own_queries, "tensor", 0)
    lower_half = jnp.where(side_index == 0, own_queries, other_queries)
    upper_half = jnp.where(side_index == 0, other_queries, own_queries)
    queries = jnp.concatenate([lower_half, upper_half], axis=1)[:, None]

    head_results = attention_kernel(
        queries[:, 0],
        dense_cache,
        new_tokens,
        lengths,
        side_index * rows_per_head,
        side_index * fresh_per,
    )
    lower, upper, maximum, denominator = head_results
    half_dim = HD // 2
    given_part = jnp.where(side_index == 0, upper, lower)
    kept_part = jnp.where(side_index == 0, lower, upper)
    received_part, other_max, other_den = swapped((given_part, maximum, denominator), "tensor", 0)
    joint_max = jnp.maximum(maximum, other_max)
    own_scale = jnp.exp(maximum - joint_max)
    theirs = jnp.exp(other_max - joint_max)
    combined = kept_part * own_scale[..., None] + received_part * theirs[..., None]
    attended = combined / (denominator * own_scale + other_den * theirs)[..., None]
    attended = attended.astype(jnp.bfloat16)
    back = [attended[0]]
    for j in range(1, group_count):
        back.append(
            lax.ppermute(attended[j], "dp", [(i, (i + j) % group_count) for i in range(group_count)])
        )
    attended = jnp.stack(back)[(group_index - source) % group_count]
    tok_rows = residual_in.shape[0]
    head_out = attended.reshape(tensor_size, tok_rows, half_dim)
    owned = lax.all_to_all(head_out, "tensor", split_axis=0, concat_axis=0, tiled=True)
    owned = owned.transpose(1, 0, 2).reshape(tok_rows, tensor_size * half_dim)
    full_weight = lax.all_gather(out_weight, "tensor", axis=0, tiled=True)
    projected = jnp.dot(owned, full_weight, preferred_element_type=jnp.float32)
    hidden = residual_in.astype(jnp.float32) + projected
    normed = (
        hidden * lax.rsqrt(jnp.mean(hidden * hidden, axis=1, keepdims=True) + 1e-06) * norm_gain
    ).astype(jnp.bfloat16)
    capacity = max(2, tok_rows * TOP * 4 // (3 * EXPERTS))
    flat_routes = routes.reshape(-1)
    pair_count = flat_routes.shape[0]
    expert_ids = jnp.arange(EXPERTS, dtype=jnp.int32)
    one_hot = (flat_routes[:, None] == expert_ids[None, :]).astype(jnp.int32)
    earlier = jnp.cumsum(one_hot, axis=0) - one_hot
    rank_in_expert = jnp.sum(earlier * one_hot, axis=1)
    slot_of_pair = flat_routes * capacity + rank_in_expert
    slot_ids = jnp.arange(EXPERTS * capacity, dtype=jnp.int32)
    matches = slot_of_pair[None, :] == slot_ids[:, None]
    source_pair = jnp.sum(
        jnp.where(matches, jnp.arange(pair_count, dtype=jnp.int32)[None, :], 0), axis=1
    )
    filled = jnp.any(matches, axis=1)
    outgoing_rows = jnp.where(
        filled[:, None], normed[source_pair // TOP], jnp.zeros((), jnp.bfloat16)
    )
    experts_here = expert_gate.shape[0]
    width = normed.shape[1]
    outgoing_rows = outgoing_rows.reshape(tensor_size, experts_here, capacity, width)
    owner_slot = (flat_routes // experts_here) * capacity + rank_in_expert
    parity = flat_routes % experts_here
    routed = jnp.zeros((tok_rows, width), jnp.float32)
    slot_ids = jnp.arange(tensor_size * capacity, dtype=jnp.int32)
    flat_gates = route_gates.reshape(-1)
    for k in range(experts_here):
        if k == 0:
            fanned = jnp.broadcast_to(outgoing_rows[None, :, k], (group_count,) + outgoing_rows[:, k].shape)
            fanned = fanned.reshape((group_count * tensor_size, capacity, width))
            arrived_rows = lax.all_to_all(
                fanned, ("dp", "tensor"), split_axis=0, concat_axis=0, tiled=True
            )
        else:
            same_group = lax.all_to_all(
                outgoing_rows[:, k], "tensor", split_axis=0, concat_axis=0, tiled=True
            )
            arrived_rows = lax.all_gather(same_group, "dp", axis=0, tiled=True)
        flat_rows = arrived_rows.reshape(-1, width)
        gate_part = jnp.dot(flat_rows, expert_gate[k], preferred_element_type=jnp.float32)
        up_part = jnp.dot(flat_rows, expert_up[k], preferred_element_type=jnp.float32)
        active = (jax.nn.silu(gate_part) * up_part).astype(jnp.bfloat16)
        partial_value = jnp.dot(active, expert_down[k], preferred_element_type=jnp.float32)
        partial_value = partial_value.astype(jnp.bfloat16).reshape(arrived_rows.shape)
        hit = (owner_slot[:, None] == slot_ids[None, :]) & (parity == k)[:, None]
        coeff = jnp.where(hit, flat_gates[:, None], 0.0).reshape(tok_rows, TOP, -1).sum(axis=1)
        if k == 0:
            returned = lax.all_to_all(
                partial_value, ("dp", "tensor"), split_axis=0, concat_axis=0, tiled=True
            )
            coeff = jnp.tile(coeff, (1, group_count))
        else:
            reduced = lax.psum_scatter(partial_value, "dp", scatter_dimension=0, tiled=True)
            returned = lax.all_to_all(reduced, "tensor", split_axis=0, concat_axis=0, tiled=True)
        routed = routed + jnp.dot(
            coeff,
            returned.reshape(-1, width).astype(jnp.float32),
            precision=lax.Precision.HIGHEST,
            preferred_element_type=jnp.float32,
        )
    return hidden + routed


def solution(mesh):
    return jax.shard_map(
        shards,
        mesh=mesh,
        in_specs=(
            P("dp", "tensor", None),
            P("dp", None),
            P(),
            P(),
            P("dp", "tensor", None),
            P(("dp", "tensor"), None),
            P("tensor", None),
            P(),
            P(("dp", "tensor"), None),
            P(("dp", "tensor"), None),
            P("tensor", None, "dp"),
            P("tensor", None, "dp"),
            P("tensor", "dp", None),
        ),
        out_specs=P(("dp", "tensor"), None),
        check_vma=False,
    )
```

```python
import functools

import jax
import jax.numpy as jnp
from jax import lax
from jax.experimental import pallas as pl
from jax.experimental.pallas import tpu as pltpu
from jax.sharding import PartitionSpec as P

HEADS = 16
HD = 128
EXPERTS = 64
TOP = 6
PAGE = 64


def swapped(array, axis, stride):
    return lax.ppermute(array, axis, [(i, i ^ 1 << stride) for i in range(lax.axis_size(axis))])


def attn_body(scal_ref, q_ref, c_ref, f_ref, lo_ref, hi_ref, m_ref, d_ref, *, block_q, page_rows, head):
    item = pl.program_id(0)
    qb = pl.program_id(1)
    length = scal_ref[item]
    cache_offset = scal_ref[4]
    span_offset = scal_ref[5]
    scale = 1.0 / head**0.5
    q = q_ref[...]
    cached = c_ref[...]
    fresh = f_ref[...]
    dims = (((1,), (1,)), ((), ()))
    cs = lax.dot_general(q, cached[:, :head], dims, preferred_element_type=jnp.float32) * scale
    n = lax.broadcasted_iota(jnp.int32, cs.shape, 1)
    pos = (n // page_rows) * PAGE + cache_offset + n % page_rows
    cs = jnp.where(pos < length, cs, -1e30)
    ss = lax.dot_general(q, fresh[:, head:2 * head], dims, preferred_element_type=jnp.float32) * scale
    kpos = span_offset + lax.broadcasted_iota(jnp.int32, ss.shape, 1)
    qpos = qb * block_q + lax.broadcasted_iota(jnp.int32, ss.shape, 0)
    ss = jnp.where(kpos <= qpos, ss, -1e30)
    mx = jnp.maximum(jnp.max(cs, axis=1, keepdims=True), jnp.max(ss, axis=1, keepdims=True))
    cw = jnp.exp(cs - mx)
    sw = jnp.exp(ss - mx)
    den = jnp.sum(cw, axis=1, keepdims=True) + jnp.sum(sw, axis=1, keepdims=True)
    acc = jnp.dot(cw.astype(jnp.bfloat16), cached[:, head:], preferred_element_type=jnp.float32)
    acc = acc + jnp.dot(sw.astype(jnp.bfloat16), fresh[:, 2 * head:], preferred_element_type=jnp.float32)
    half = head // 2
    lo_ref[...] = acc[:, :half]
    hi_ref[...] = acc[:, half:]
    m_ref[...] = jnp.transpose(jnp.broadcast_to(mx, (block_q, 128)))[0:1, :]
    d_ref[...] = jnp.transpose(jnp.broadcast_to(den, (block_q, 128)))[0:1, :]


def attention_kernel(queries, cached, fresh, lengths, cache_offset, span_offset, interpret=False):
    items, span, head = queries.shape
    pages, page_rows = cached.shape[1], cached.shape[2]
    keys = pages * page_rows
    cached = cached.reshape(items, keys, cached.shape[3])
    fresh_rows = fresh.shape[1]
    block_q = 256
    scal = jnp.concatenate(
        [lengths.astype(jnp.int32), jnp.stack([cache_offset, span_offset]).astype(jnp.int32)]
    )
    body = functools.partial(attn_body, block_q=block_q, page_rows=page_rows, head=head)
    grid_spec = pltpu.PrefetchScalarGridSpec(
        num_scalar_prefetch=1,
        grid=(items, span // block_q),
        in_specs=[
            pl.BlockSpec((None, block_q, head), lambda i, b, s: (i, b, 0)),
            pl.BlockSpec((None, keys, 2 * head), lambda i, b, s: (i, 0, 0)),
            pl.BlockSpec((None, fresh_rows, 3 * head), lambda i, b, s: (i, 0, 0)),
        ],
        out_specs=[
            pl.BlockSpec((None, block_q, head // 2), lambda i, b, s: (i, b, 0)),
            pl.BlockSpec((None, block_q, head // 2), lambda i, b, s: (i, b, 0)),
            pl.BlockSpec((None, 1, block_q), lambda i, b, s: (i, 0, b)),
            pl.BlockSpec((None, 1, block_q), lambda i, b, s: (i, 0, b)),
        ],
    )
    lower, upper, mx, den = pl.pallas_call(
        body,
        grid_spec=grid_spec,
        out_shape=[
            jax.ShapeDtypeStruct((items, span, head // 2), jnp.float32),
            jax.ShapeDtypeStruct((items, span, head // 2), jnp.float32),
            jax.ShapeDtypeStruct((items, 1, span), jnp.float32),
            jax.ShapeDtypeStruct((items, 1, span), jnp.float32),
        ],
        interpret=interpret,
    )(scal, queries, cached, fresh)
    return lower, upper, mx[:, 0], den[:, 0]


def run_experts(slot_rows, expert_gate, expert_up, expert_down):
    gate_part = jnp.einsum(
        "secd,edf->secf", slot_rows, expert_gate, preferred_element_type=jnp.float32
    )
    up_part = jnp.einsum("secd,edf->secf", slot_rows, expert_up, preferred_element_type=jnp.float32)
    active = (jax.nn.silu(gate_part) * up_part).astype(jnp.bfloat16)
    return jnp.einsum("secf,efd->secd", active, expert_down, preferred_element_type=jnp.float32)


def shards(
    page_pool,
    page_table,
    destination,
    cache_len,
    new_tokens,
    residual_in,
    out_weight,
    norm_gain,
    routes,
    route_gates,
    expert_gate,
    expert_up,
    expert_down,
):
    tensor_size = lax.axis_size("tensor")
    group_count = lax.axis_size("dp")
    split_ways = max(1, tensor_size // HEADS)
    heads_here = max(1, HEADS // tensor_size)
    side_index = lax.axis_index("tensor") % split_ways
    group_index = lax.axis_index("dp")
    requests_here = page_table.shape[0]
    first_home = group_index * requests_here
    home_dest = lax.dynamic_slice_in_dim(destination, first_home, requests_here)
    dest_group = home_dest // requests_here
    request_ids = jnp.arange(requests_here, dtype=jnp.int32)
    shifts = jnp.arange(group_count, dtype=jnp.int32)
    work_req = jnp.sum(
        jnp.where(
            dest_group[None, :] == (group_index + shifts[:, None]) % group_count,
            request_ids[None, :],
            0,
        ),
        axis=1,
    )
    inverse = (
        jnp.zeros_like(destination)
        .at[destination]
        .set(jnp.arange(destination.shape[0], dtype=jnp.int32))
    )
    served = lax.dynamic_slice_in_dim(inverse, first_home, requests_here)
    source = served // requests_here
    send_slot = jnp.sum(
        jnp.where(
            source[None, :] == (group_index - shifts[:, None]) % group_count,
            request_ids[None, :],
            0,
        ),
        axis=1,
    )
    outgoing_tokens = new_tokens[send_slot]
    fresh = [outgoing_tokens[0]]
    for j in range(1, group_count):
        fresh.append(
            lax.ppermute(
                outgoing_tokens[j], "dp", [(i, (i - j) % group_count) for i in range(group_count)]
            )
        )
    new_tokens = jnp.stack(fresh)
    dense_cache = page_pool[page_table[work_req]]
    lengths = cache_len[first_home + work_req]
    fresh_per = new_tokens.shape[1] // heads_here
    span_len = fresh_per * split_ways
    rows_per_head = dense_cache.shape[2] // heads_here
    own_queries = new_tokens[:, :, :HD]
    other_queries = swapped(own_queries, "tensor", 0)
    lower_half = jnp.where(side_index == 0, own_queries, other_queries)
    upper_half = jnp.where(side_index == 0, other_queries, own_queries)
    queries = jnp.concatenate([lower_half, upper_half], axis=1)[:, None]

    head_results = attention_kernel(
        queries[:, 0],
        dense_cache,
        new_tokens,
        lengths,
        side_index * rows_per_head,
        side_index * fresh_per,
    )
    lower, upper, maximum, denominator = head_results
    half_dim = HD // 2
    given_part = jnp.where(side_index == 0, upper, lower)
    kept_part = jnp.where(side_index == 0, lower, upper)
    received_part, other_max, other_den = swapped((given_part, maximum, denominator), "tensor", 0)
    joint_max = jnp.maximum(maximum, other_max)
    own_scale = jnp.exp(maximum - joint_max)
    theirs = jnp.exp(other_max - joint_max)
    combined = kept_part * own_scale[..., None] + received_part * theirs[..., None]
    attended = combined / (denominator * own_scale + other_den * theirs)[..., None]
    attended = attended.astype(jnp.bfloat16)
    back = [attended[0]]
    for j in range(1, group_count):
        back.append(
            lax.ppermute(attended[j], "dp", [(i, (i + j) % group_count) for i in range(group_count)])
        )
    attended = jnp.stack(back)[(group_index - source) % group_count]
    tok_rows = residual_in.shape[0]
    head_out = attended.reshape(tensor_size, tok_rows, half_dim)
    owned = lax.all_to_all(head_out, "tensor", split_axis=0, concat_axis=0, tiled=True)
    owned = owned.transpose(1, 0, 2).reshape(tok_rows, tensor_size * half_dim)
    full_weight = lax.all_gather(out_weight, "tensor", axis=0, tiled=True)
    projected = jnp.dot(owned, full_weight, preferred_element_type=jnp.float32)
    hidden = residual_in.astype(jnp.float32) + projected
    normed = (
        hidden * lax.rsqrt(jnp.mean(hidden * hidden, axis=1, keepdims=True) + 1e-06) * norm_gain
    ).astype(jnp.bfloat16)
    capacity = max(2, tok_rows * TOP * 4 // (3 * EXPERTS))
    flat_routes = routes.reshape(-1)
    pair_count = flat_routes.shape[0]
    expert_ids = jnp.arange(EXPERTS, dtype=jnp.int32)
    one_hot = (flat_routes[:, None] == expert_ids[None, :]).astype(jnp.int32)
    earlier = jnp.cumsum(one_hot, axis=0) - one_hot
    rank_in_expert = jnp.sum(earlier * one_hot, axis=1)
    slot_of_pair = flat_routes * capacity + rank_in_expert
    slot_ids = jnp.arange(EXPERTS * capacity, dtype=jnp.int32)
    matches = slot_of_pair[None, :] == slot_ids[:, None]
    source_pair = jnp.sum(
        jnp.where(matches, jnp.arange(pair_count, dtype=jnp.int32)[None, :], 0), axis=1
    )
    filled = jnp.any(matches, axis=1)
    outgoing_rows = jnp.where(
        filled[:, None], normed[source_pair // TOP], jnp.zeros((), jnp.bfloat16)
    )
    experts_here = expert_gate.shape[0]
    width = normed.shape[1]
    outgoing_rows = outgoing_rows.reshape(tensor_size, experts_here, capacity, width)
    owner_slot = (flat_routes // experts_here) * capacity + rank_in_expert
    parity = flat_routes % experts_here
    routed = jnp.zeros((tok_rows, width), jnp.float32)
    slot_ids = jnp.arange(tensor_size * capacity, dtype=jnp.int32)
    flat_gates = route_gates.reshape(-1)
    for k in range(experts_here):
        if k == 1:
            fanned = jnp.broadcast_to(outgoing_rows[None, :, k], (group_count,) + outgoing_rows[:, k].shape)
            fanned = fanned.reshape((group_count * tensor_size, capacity, width))
            arrived_rows = lax.all_to_all(
                fanned, ("dp", "tensor"), split_axis=0, concat_axis=0, tiled=True
            )
        else:
            same_group = lax.all_to_all(
                outgoing_rows[:, k], "tensor", split_axis=0, concat_axis=0, tiled=True
            )
            arrived_rows = lax.all_gather(same_group, "dp", axis=0, tiled=True)
        flat_rows = arrived_rows.reshape(-1, width)
        gate_part = jnp.dot(flat_rows, expert_gate[k], preferred_element_type=jnp.float32)
        up_part = jnp.dot(flat_rows, expert_up[k], preferred_element_type=jnp.float32)
        active = (jax.nn.silu(gate_part) * up_part).astype(jnp.bfloat16)
        partial_value = jnp.dot(active, expert_down[k], preferred_element_type=jnp.float32)
        partial_value = partial_value.astype(jnp.bfloat16).reshape(arrived_rows.shape)
        reduced = lax.psum_scatter(partial_value, "dp", scatter_dimension=0, tiled=True)
        returned = lax.all_to_all(reduced, "tensor", split_axis=0, concat_axis=0, tiled=True)
        hit = (owner_slot[:, None] == slot_ids[None, :]) & (parity == k)[:, None]
        coeff = jnp.where(hit, flat_gates[:, None], 0.0).reshape(tok_rows, TOP, -1).sum(axis=1)
        routed = routed + jnp.dot(
            coeff,
            returned.reshape(-1, width).astype(jnp.float32),
            precision=lax.Precision.HIGHEST,
            preferred_element_type=jnp.float32,
        )
    return hidden + routed


def solution(mesh):
    return jax.shard_map(
        shards,
        mesh=mesh,
        in_specs=(
            P("dp", "tensor", None),
            P("dp", None),
            P(),
            P(),
            P("dp", "tensor", None),
            P(("dp", "tensor"), None),
            P("tensor", None),
            P(),
            P(("dp", "tensor"), None),
            P(("dp", "tensor"), None),
            P("tensor", None, "dp"),
            P("tensor", None, "dp"),
            P("tensor", "dp", None),
        ),
        out_specs=P(("dp", "tensor"), None),
        check_vma=False,
    )
```

```python
import functools

import jax
import jax.numpy as jnp
from jax import lax
from jax.experimental import pallas as pl
from jax.experimental.pallas import tpu as pltpu
from jax.sharding import PartitionSpec as P

HEADS = 16
HD = 128
EXPERTS = 64
TOP = 6
PAGE = 64


def swapped(array, axis, stride):
    return lax.ppermute(array, axis, [(i, i ^ 1 << stride) for i in range(lax.axis_size(axis))])


def attn_body(scal_ref, q_ref, c_ref, f_ref, lo_ref, hi_ref, m_ref, d_ref, *, items, block_q, page_rows, head):
    item = pl.program_id(0)
    qb = pl.program_id(1)
    length = scal_ref[item]
    cache_offset = scal_ref[items]
    span_offset = scal_ref[items + 1]
    scale = 1.0 / head**0.5
    q = q_ref[...]
    cached = c_ref[...]
    fresh = f_ref[...]
    dims = (((1,), (1,)), ((), ()))
    cs = lax.dot_general(q, cached[:, :head], dims, preferred_element_type=jnp.float32) * scale
    n = lax.broadcasted_iota(jnp.int32, cs.shape, 1)
    pos = (n // page_rows) * PAGE + cache_offset + n % page_rows
    cs = jnp.where(pos < length, cs, -1e30)
    ss = lax.dot_general(q, fresh[:, head:2 * head], dims, preferred_element_type=jnp.float32) * scale
    kpos = span_offset + lax.broadcasted_iota(jnp.int32, ss.shape, 1)
    qpos = qb * block_q + lax.broadcasted_iota(jnp.int32, ss.shape, 0)
    ss = jnp.where(kpos <= qpos, ss, -1e30)
    mx = jnp.maximum(jnp.max(cs, axis=1, keepdims=True), jnp.max(ss, axis=1, keepdims=True))
    cw = jnp.exp(cs - mx)
    sw = jnp.exp(ss - mx)
    den = jnp.sum(cw, axis=1, keepdims=True) + jnp.sum(sw, axis=1, keepdims=True)
    acc = jnp.dot(cw.astype(jnp.bfloat16), cached[:, head:], preferred_element_type=jnp.float32)
    acc = acc + jnp.dot(sw.astype(jnp.bfloat16), fresh[:, 2 * head:], preferred_element_type=jnp.float32)
    half = head // 2
    lo_ref[...] = acc[:, :half]
    hi_ref[...] = acc[:, half:]
    m_ref[...] = jnp.transpose(jnp.broadcast_to(mx, (block_q, 128)))[0:1, :]
    d_ref[...] = jnp.transpose(jnp.broadcast_to(den, (block_q, 128)))[0:1, :]


def attention_kernel(queries, cached, fresh, lengths, cache_offset, span_offset, interpret=False):
    items, span, head = queries.shape
    pages, page_rows = cached.shape[1], cached.shape[2]
    keys = pages * page_rows
    cached = cached.reshape(items, keys, cached.shape[3])
    fresh_rows = fresh.shape[1]
    block_q = 256
    scal = jnp.concatenate(
        [lengths.astype(jnp.int32), jnp.stack([cache_offset, span_offset]).astype(jnp.int32)]
    )
    body = functools.partial(attn_body, items=items, block_q=block_q, page_rows=page_rows, head=head)
    grid_spec = pltpu.PrefetchScalarGridSpec(
        num_scalar_prefetch=1,
        grid=(items, span // block_q),
        in_specs=[
            pl.BlockSpec((None, block_q, head), lambda i, b, s: (i, b, 0)),
            pl.BlockSpec((None, keys, 2 * head), lambda i, b, s: (i, 0, 0)),
            pl.BlockSpec((None, fresh_rows, 3 * head), lambda i, b, s: (i, 0, 0)),
        ],
        out_specs=[
            pl.BlockSpec((None, block_q, head // 2), lambda i, b, s: (i, b, 0)),
            pl.BlockSpec((None, block_q, head // 2), lambda i, b, s: (i, b, 0)),
            pl.BlockSpec((None, 1, block_q), lambda i, b, s: (i, 0, b)),
            pl.BlockSpec((None, 1, block_q), lambda i, b, s: (i, 0, b)),
        ],
    )
    lower, upper, mx, den = pl.pallas_call(
        body,
        grid_spec=grid_spec,
        out_shape=[
            jax.ShapeDtypeStruct((items, span, head // 2), jnp.float32),
            jax.ShapeDtypeStruct((items, span, head // 2), jnp.float32),
            jax.ShapeDtypeStruct((items, 1, span), jnp.float32),
            jax.ShapeDtypeStruct((items, 1, span), jnp.float32),
        ],
        interpret=interpret,
    )(scal, queries, cached, fresh)
    return lower, upper, mx[:, 0], den[:, 0]


def run_experts(slot_rows, expert_gate, expert_up, expert_down):
    gate_part = jnp.einsum(
        "secd,edf->secf", slot_rows, expert_gate, preferred_element_type=jnp.float32
    )
    up_part = jnp.einsum("secd,edf->secf", slot_rows, expert_up, preferred_element_type=jnp.float32)
    active = (jax.nn.silu(gate_part) * up_part).astype(jnp.bfloat16)
    return jnp.einsum("secf,efd->secd", active, expert_down, preferred_element_type=jnp.float32)


def shards(
    page_pool,
    page_table,
    destination,
    cache_len,
    new_tokens,
    residual_in,
    out_weight,
    norm_gain,
    routes,
    route_gates,
    expert_gate,
    expert_up,
    expert_down,
):
    tensor_size = lax.axis_size("tensor")
    group_count = lax.axis_size("dp")
    split_ways = max(1, tensor_size // HEADS)
    heads_here = max(1, HEADS // tensor_size)
    side_index = lax.axis_index("tensor") % split_ways
    group_index = lax.axis_index("dp")
    requests_here = page_table.shape[0]
    first_home = group_index * requests_here
    home_dest = lax.dynamic_slice_in_dim(destination, first_home, requests_here)
    dest_group = home_dest // requests_here
    request_ids = jnp.arange(requests_here, dtype=jnp.int32)
    shifts = jnp.arange(group_count, dtype=jnp.int32)
    work_req = jnp.sum(
        jnp.where(
            dest_group[None, :] == (group_index + shifts[:, None]) % group_count,
            request_ids[None, :],
            0,
        ),
        axis=1,
    )
    inverse = (
        jnp.zeros_like(destination)
        .at[destination]
        .set(jnp.arange(destination.shape[0], dtype=jnp.int32))
    )
    served = lax.dynamic_slice_in_dim(inverse, first_home, requests_here)
    source = served // requests_here
    send_slot = jnp.sum(
        jnp.where(
            source[None, :] == (group_index - shifts[:, None]) % group_count,
            request_ids[None, :],
            0,
        ),
        axis=1,
    )
    outgoing_tokens = new_tokens[send_slot]
    fresh = [outgoing_tokens[0]]
    for j in range(1, group_count):
        fresh.append(
            lax.ppermute(
                outgoing_tokens[j], "dp", [(i, (i - j) % group_count) for i in range(group_count)]
            )
        )
    new_tokens = jnp.stack(fresh)
    dense_cache = page_pool[page_table[work_req]]
    lengths = cache_len[first_home + work_req]
    fresh_per = new_tokens.shape[1] // heads_here
    span_len = fresh_per * split_ways
    rows_per_head = dense_cache.shape[2] // heads_here
    def run_items(fresh_items, cache_items, length_items):
        own_queries = fresh_items[:, :, :HD]
        other_queries = swapped(own_queries, "tensor", 0)
        lower_half = jnp.where(side_index == 0, own_queries, other_queries)
        upper_half = jnp.where(side_index == 0, other_queries, own_queries)
        queries = jnp.concatenate([lower_half, upper_half], axis=1)
        return attention_kernel(
            queries,
            cache_items,
            fresh_items,
            length_items,
            side_index * rows_per_head,
            side_index * fresh_per,
        )

    local_part = run_items(new_tokens[:1], dense_cache[:1], lengths[:1])
    moved_part = run_items(new_tokens[1:], dense_cache[1:], lengths[1:])
    head_results = [jnp.concatenate([x, y], axis=0) for x, y in zip(local_part, moved_part)]
    lower, upper, maximum, denominator = head_results
    half_dim = HD // 2
    given_part = jnp.where(side_index == 0, upper, lower)
    kept_part = jnp.where(side_index == 0, lower, upper)
    received_part, other_max, other_den = swapped((given_part, maximum, denominator), "tensor", 0)
    joint_max = jnp.maximum(maximum, other_max)
    own_scale = jnp.exp(maximum - joint_max)
    theirs = jnp.exp(other_max - joint_max)
    combined = kept_part * own_scale[..., None] + received_part * theirs[..., None]
    attended = combined / (denominator * own_scale + other_den * theirs)[..., None]
    attended = attended.astype(jnp.bfloat16)
    back = [attended[0]]
    for j in range(1, group_count):
        back.append(
            lax.ppermute(attended[j], "dp", [(i, (i + j) % group_count) for i in range(group_count)])
        )
    attended = jnp.stack(back)[(group_index - source) % group_count]
    tok_rows = residual_in.shape[0]
    head_out = attended.reshape(tensor_size, tok_rows, half_dim)
    owned = lax.all_to_all(head_out, "tensor", split_axis=0, concat_axis=0, tiled=True)
    owned = owned.transpose(1, 0, 2).reshape(tok_rows, tensor_size * half_dim)
    full_weight = lax.all_gather(out_weight, "tensor", axis=0, tiled=True)
    projected = jnp.dot(owned, full_weight, preferred_element_type=jnp.float32)
    hidden = residual_in.astype(jnp.float32) + projected
    normed = (
        hidden * lax.rsqrt(jnp.mean(hidden * hidden, axis=1, keepdims=True) + 1e-06) * norm_gain
    ).astype(jnp.bfloat16)
    capacity = max(2, tok_rows * TOP * 4 // (3 * EXPERTS))
    flat_routes = routes.reshape(-1)
    pair_count = flat_routes.shape[0]
    expert_ids = jnp.arange(EXPERTS, dtype=jnp.int32)
    one_hot = (flat_routes[:, None] == expert_ids[None, :]).astype(jnp.int32)
    earlier = jnp.cumsum(one_hot, axis=0) - one_hot
    rank_in_expert = jnp.sum(earlier * one_hot, axis=1)
    slot_of_pair = flat_routes * capacity + rank_in_expert
    slot_ids = jnp.arange(EXPERTS * capacity, dtype=jnp.int32)
    matches = slot_of_pair[None, :] == slot_ids[:, None]
    source_pair = jnp.sum(
        jnp.where(matches, jnp.arange(pair_count, dtype=jnp.int32)[None, :], 0), axis=1
    )
    filled = jnp.any(matches, axis=1)
    outgoing_rows = jnp.where(
        filled[:, None], normed[source_pair // TOP], jnp.zeros((), jnp.bfloat16)
    )
    experts_here = expert_gate.shape[0]
    width = normed.shape[1]
    outgoing_rows = outgoing_rows.reshape(tensor_size, experts_here, capacity, width)
    owner_slot = (flat_routes // experts_here) * capacity + rank_in_expert
    parity = flat_routes % experts_here
    routed = jnp.zeros((tok_rows, width), jnp.float32)
    slot_ids = jnp.arange(tensor_size * capacity, dtype=jnp.int32)
    flat_gates = route_gates.reshape(-1)
    for k in range(experts_here):
        if k == 0:
            fanned = jnp.broadcast_to(outgoing_rows[None, :, k], (group_count,) + outgoing_rows[:, k].shape)
            fanned = fanned.reshape((group_count * tensor_size, capacity, width))
            arrived_rows = lax.all_to_all(
                fanned, ("dp", "tensor"), split_axis=0, concat_axis=0, tiled=True
            )
        else:
            same_group = lax.all_to_all(
                outgoing_rows[:, k], "tensor", split_axis=0, concat_axis=0, tiled=True
            )
            arrived_rows = lax.all_gather(same_group, "dp", axis=0, tiled=True)
        flat_rows = arrived_rows.reshape(-1, width)
        gate_part = jnp.dot(flat_rows, expert_gate[k], preferred_element_type=jnp.float32)
        up_part = jnp.dot(flat_rows, expert_up[k], preferred_element_type=jnp.float32)
        active = (jax.nn.silu(gate_part) * up_part).astype(jnp.bfloat16)
        partial_value = jnp.dot(active, expert_down[k], preferred_element_type=jnp.float32)
        partial_value = partial_value.astype(jnp.bfloat16).reshape(arrived_rows.shape)
        reduced = lax.psum_scatter(partial_value, "dp", scatter_dimension=0, tiled=True)
        returned = lax.all_to_all(reduced, "tensor", split_axis=0, concat_axis=0, tiled=True)
        hit = (owner_slot[:, None] == slot_ids[None, :]) & (parity == k)[:, None]
        coeff = jnp.where(hit, flat_gates[:, None], 0.0).reshape(tok_rows, TOP, -1).sum(axis=1)
        routed = routed + jnp.dot(
            coeff,
            returned.reshape(-1, width).astype(jnp.float32),
            precision=lax.Precision.HIGHEST,
            preferred_element_type=jnp.float32,
        )
    return hidden + routed


def solution(mesh):
    return jax.shard_map(
        shards,
        mesh=mesh,
        in_specs=(
            P("dp", "tensor", None),
            P("dp", None),
            P(),
            P(),
            P("dp", "tensor", None),
            P(("dp", "tensor"), None),
            P("tensor", None),
            P(),
            P(("dp", "tensor"), None),
            P(("dp", "tensor"), None),
            P("tensor", None, "dp"),
            P("tensor", None, "dp"),
            P("tensor", "dp", None),
        ),
        out_specs=P(("dp", "tensor"), None),
        check_vma=False,
    )
```
